256 devices in a mesh: gx: 16 (over y_lo, z), gy: 16 (over y_hi, x, core).
Axes of the slice: x: 4, y: 4 (y_hi: 2, y_lo: 2; y = y_hi * 2 + y_lo), z: 8, core: 2. Of those that a mesh axis runs over, the one named last changes fastest.
Arguments:
- initial_warmth_field: float32 [16, 2048, 2048], P(None, 'gx', 'gy'), may hold values from -8 to 8
- horizontal_motion_pair: float32 [2, 16, 2048, 2048], P(None, None, 'gx', 'gy'), may hold values from -4 to 4
- z_directed_motion: float32 [16, 2048, 2048], P(None, 'gx', 'gy'), may hold values from -3 to 3
- earlier_rate_change: float32 [16, 2048, 2048], P(None, 'gx', 'gy'), may hold values from -6 to 6
- layer_depth_spacing: float32 [16], replicated, may hold values from 0.5 to 2
- backward_spread_ratio: float32 [16], replicated, may hold values from 4 to 100000
- wall_warmth_bounds: float32 [2, 2048, 2048], P(None, 'gx', 'gy'), may hold values from -4 to 4
Outputs:
- resulting_warmth_field: float32 [16, 2048, 2048], P(None, 'gx', 'gy')
- current_rate_change: float32 [16, 2048, 2048], P(None, 'gx', 'gy')
The draws below stay inside these ranges and needn't reach their ends.
All inputs are finite; a program needn't handle non-finite values.
Results may differ from the reference program's by a relative error of at most 0.000071.
Values sent between devices are 32-bit elements; how exact they have to be, the bound alone decides.
No kernel may reach another device: no remote copies, remote signals or barrier semaphores. Data moves between devices by JAX's collectives and lax.ppermute only.
A program may use at most 64 MiB of HBM per device.

```python
import math
import jax
import jax.numpy as jnp

NZ = 16
CELLS_ALONG_X = 2048
CELLS_ALONG_Y = 2048


def draw_initial_warmth_field(key, part):
    key_rough = jax.random.fold_in(key, 0)
    return jnp.clip(jax.random.normal(key_rough, (NZ, CELLS_ALONG_X, CELLS_ALONG_Y), jnp.float32), -6.0, 6.0)


def draw_backward_spread_ratio(key, part):
    exponent = jax.random.uniform(key, (NZ,), jnp.float32, math.log(4.0), math.log(100000.0))
    return jnp.clip(jnp.exp(exponent), 4.0, 100000.0)


def block_scale(key, extent, cuts, least, top_value):
    gain = 1.0
    for dim, blocks in cuts:
        heights = jax.random.uniform(jax.random.fold_in(jax.random.fold_in(key, 6), dim), (blocks,), jnp.float32, least / len(cuts), top_value / len(cuts))
        gain = gain * jnp.repeat(jnp.exp(heights), extent[dim] // blocks).reshape((-1,) + (1,) * (len(extent) - 1 - dim))
    return gain


def centred(key, extent, width, most, cuts=(), kind=jnp.bfloat16):
    result = jax.random.normal(key, extent, jnp.float32) * width
    if len(cuts) > 0:
        result = block_scale(key, extent, cuts, -0.22, 0.18) * result
    return jnp.clip(result, min=-most, max=most).astype(kind)


def setup_inputs(seed: int = 0) -> dict:
    key_list = jax.random.split(jax.random.key(seed), 8)
    return {
        "initial_warmth_field": draw_initial_warmth_field(jax.random.fold_in(key_list[7], 71), 0),
        "horizontal_motion_pair": centred(key_list[1], (2, NZ, CELLS_ALONG_X, CELLS_ALONG_Y), 1.0, 4.0, ((2, 16), (3, 16)), jnp.float32),
        "z_directed_motion": centred(key_list[2], (NZ, CELLS_ALONG_X, CELLS_ALONG_Y), 0.5, 3.0, ((1, 16), (2, 16)), jnp.float32),
        "earlier_rate_change": centred(key_list[3], (NZ, CELLS_ALONG_X, CELLS_ALONG_Y), 1.0, 6.0, ((1, 16), (2, 16)), jnp.float32),
        "layer_depth_spacing": jnp.clip(jnp.exp(jax.random.uniform(key_list[4], (NZ,), jnp.float32, math.log(0.5), math.log(2.0))), 0.5, 2.0),
        "backward_spread_ratio": draw_backward_spread_ratio(jax.random.fold_in(key_list[7], 71), 0),
        "wall_warmth_bounds": centred(key_list[6], (2, CELLS_ALONG_X, CELLS_ALONG_Y), 1.0, 4.0, ((1, 16), (2, 16)), jnp.float32),
    }


COURANT = 0.5
DIFF_Y = 0.2
DIFF_Z = 0.25
NEW_TERM_COEF = 0.75
OLD_TERM_COEF = -5.0 / 12.0


def depthwise_rate_change(initial_warmth_field, z_directed_motion, layer_depth_spacing, wall_warmth_bounds):
    inner_face_transport = (z_directed_motion[:-1] + z_directed_motion[1:]) * (initial_warmth_field[:-1] + initial_warmth_field[1:]) * 0.25
    empty_layer_sheet = jnp.zeros_like(initial_warmth_field[:1])
    flux_up = jnp.concatenate([empty_layer_sheet, inner_face_transport, empty_layer_sheet], 0)
    spacing = layer_depth_spacing[:, None, None]
    carry_through_depth = (flux_up[1:] - flux_up[:-1]) / spacing
    warmth_with_ghosts = jnp.concatenate([wall_warmth_bounds[:1], initial_warmth_field, wall_warmth_bounds[1:]], 0)
    midway_average = jnp.concatenate([layer_depth_spacing[:1], 0.5 * (layer_depth_spacing[:-1] + layer_depth_spacing[1:]), layer_depth_spacing[-1:]], 0)
    gradient_at_faces = (warmth_with_ghosts[1:] - warmth_with_ghosts[:-1]) / midway_average[:, None, None]
    thermal_spreading_step = (gradient_at_faces[1:] - gradient_at_faces[:-1]) / spacing
    return carry_through_depth, thermal_spreading_step


def reference(initial_warmth_field, horizontal_motion_pair, z_directed_motion, earlier_rate_change, layer_depth_spacing, backward_spread_ratio, wall_warmth_bounds):
    x_directed_motion = horizontal_motion_pair[0]
    y_directed_motion = horizontal_motion_pair[1]
    x_directed_transport = (x_directed_motion + jnp.roll(x_directed_motion, -1, 1)) * (initial_warmth_field + jnp.roll(initial_warmth_field, -1, 1)) * 0.25
    y_directed_transport = (y_directed_motion + jnp.roll(y_directed_motion, -1, 2)) * (initial_warmth_field + jnp.roll(initial_warmth_field, -1, 2)) * 0.25
    advect_xy = (x_directed_transport - jnp.roll(x_directed_transport, 1, 1)) + (y_directed_transport - jnp.roll(y_directed_transport, 1, 2))
    carry_through_depth, thermal_spreading_step = depthwise_rate_change(initial_warmth_field, z_directed_motion, layer_depth_spacing, wall_warmth_bounds)
    stacked_layer_count = jnp.roll(initial_warmth_field, -1, 2) - 2.0 * initial_warmth_field + jnp.roll(initial_warmth_field, 1, 2)
    current_rate_change = -COURANT * (advect_xy + carry_through_depth) + DIFF_Y * stacked_layer_count + DIFF_Z * thermal_spreading_step
    linear_system_source = initial_warmth_field + NEW_TERM_COEF * current_rate_change + OLD_TERM_COEF * earlier_rate_change
    cyclic_row_extent = linear_system_source.shape[1]
    spectral_coefficients = jnp.fft.rfft(linear_system_source, axis=1)
    angle_step = jnp.arange(cyclic_row_extent // 2 + 1, dtype=jnp.float32) * (math.pi / cyclic_row_extent)
    spectral_symbol = 1.0 + 4.0 * backward_spread_ratio[:, None, None] * (jnp.sin(angle_step) ** 2)[None, :, None]
    resulting_warmth_field = jnp.fft.irfft(spectral_coefficients / spectral_symbol, n=cyclic_row_extent, axis=1).astype(jnp.float32)
    return resulting_warmth_field, current_rate_change
```

```python
import jax
import jax.numpy as jnp
from jax import lax
from jax.sharding import PartitionSpec as P

COURANT = 0.5
DIFF_Y = 0.2
DIFF_Z = 0.25
NEW_TERM_COEF = 0.75
OLD_TERM_COEF = -5.0 / 12.0


def ring_pairs(count, step):
    return [(i, (i + step) % count) for i in range(count)]


def exchange_edges(first, last, axis):
    count = lax.axis_size(axis)
    from_prev = lax.ppermute(last, axis, ring_pairs(count, 1))
    from_next = lax.ppermute(first, axis, ring_pairs(count, -1))
    return from_prev, from_next


def shifted(a, halo, axis, step):
    n = a.shape[axis]
    halo = jnp.expand_dims(halo, axis)
    if step > 0:
        return jnp.concatenate([lax.slice_in_dim(a, 1, n, axis=axis), halo], axis)
    return jnp.concatenate([halo, lax.slice_in_dim(a, 0, n - 1, axis=axis)], axis)


def depthwise_rate_change(
    initial_warmth_field, z_directed_motion, layer_depth_spacing, wall_warmth_bounds
):
    inner_face_transport = (
        (z_directed_motion[:-1] + z_directed_motion[1:])
        * (initial_warmth_field[:-1] + initial_warmth_field[1:])
        * 0.25
    )
    empty_layer_sheet = jnp.zeros_like(initial_warmth_field[:1])
    flux_up = jnp.concatenate([empty_layer_sheet, inner_face_transport, empty_layer_sheet], 0)
    spacing = layer_depth_spacing[:, None, None]
    carry_through_depth = (flux_up[1:] - flux_up[:-1]) / spacing
    warmth_with_ghosts = jnp.concatenate(
        [wall_warmth_bounds[:1], initial_warmth_field, wall_warmth_bounds[1:]], 0
    )
    midway_average = jnp.concatenate(
        [
            layer_depth_spacing[:1],
            0.5 * (layer_depth_spacing[:-1] + layer_depth_spacing[1:]),
            layer_depth_spacing[-1:],
        ],
        0,
    )
    gradient_at_faces = (warmth_with_ghosts[1:] - warmth_with_ghosts[:-1]) / midway_average[
        :, None, None
    ]
    thermal_spreading_step = (gradient_at_faces[1:] - gradient_at_faces[:-1]) / spacing
    return (carry_through_depth, thermal_spreading_step)


def periodic_solve(source, ratio):
    levels, rows, cols = source.shape
    parts = lax.axis_size("gx")
    me = lax.axis_index("gx")
    root = jnp.sqrt(1.0 + 4.0 * ratio)
    mu = (1.0 + root) / ((1.0 + 2.0 * ratio) + root)
    log_lam = jnp.log1p(-mu)[:, None]

    idx = jnp.arange(rows, dtype=jnp.float32)
    to_end = jnp.exp(log_lam * (rows - 1 - idx)[None, :])
    from_start = jnp.exp(log_lam * idx[None, :])
    ends = jnp.stack(
        [
            jnp.sum(to_end[:, :, None] * source, axis=1),
            jnp.sum(from_start[:, :, None] * source, axis=1),
        ]
    )
    gathered = lax.all_gather(ends, "gx", axis=0)

    dist = jnp.abs(idx[:, None] - idx[None, :])
    kernel = jnp.exp(log_lam[:, :, None] * dist[None])
    local = jnp.einsum(
        "kij,kjc->kic", kernel, source, precision=lax.Precision.HIGHEST
    )

    others = jnp.arange(parts)
    whole = -jnp.expm1(log_lam * (parts * rows))
    lag_f = ((me - others - 1) % parts).astype(jnp.float32) * rows
    lag_b = ((others - me - 1) % parts).astype(jnp.float32) * rows
    weight_f = jnp.exp(log_lam * lag_f[None, :]) / whole
    weight_b = jnp.exp(log_lam * lag_b[None, :]) / whole
    carry_f = jnp.sum(weight_f.T[:, :, None] * gathered[:, 0], axis=0)
    carry_b = jnp.sum(weight_b.T[:, :, None] * gathered[:, 1], axis=0)
    into_f = jnp.exp(log_lam * (idx + 1.0)[None, :])
    into_b = jnp.exp(log_lam * (rows - idx)[None, :])
    total = (
        local
        + into_f[:, :, None] * carry_f[:, None, :]
        + into_b[:, :, None] * carry_b[:, None, :]
    )
    return total / root[:, None, None]


def on_device(
    initial_warmth_field,
    horizontal_motion_pair,
    z_directed_motion,
    earlier_rate_change,
    layer_depth_spacing,
    backward_spread_ratio,
    wall_warmth_bounds,
):
    t = initial_warmth_field
    u = horizontal_motion_pair[0]
    v = horizontal_motion_pair[1]
    x_prev, x_next = exchange_edges(
        jnp.stack([t[:, 0, :], u[:, 0, :]]), jnp.stack([t[:, -1, :], u[:, -1, :]]), "gx"
    )
    y_prev, y_next = exchange_edges(
        jnp.stack([t[:, :, 0], v[:, :, 0]]), jnp.stack([t[:, :, -1], v[:, :, -1]]), "gy"
    )
    t_xn = shifted(t, x_next[0], 1, 1)
    t_xp = shifted(t, x_prev[0], 1, -1)
    u_xn = shifted(u, x_next[1], 1, 1)
    u_xp = shifted(u, x_prev[1], 1, -1)
    t_yn = shifted(t, y_next[0], 2, 1)
    t_yp = shifted(t, y_prev[0], 2, -1)
    v_yn = shifted(v, y_next[1], 2, 1)
    v_yp = shifted(v, y_prev[1], 2, -1)

    flux_x_hi = (u + u_xn) * (t + t_xn) * 0.25
    flux_x_lo = (u_xp + u) * (t_xp + t) * 0.25
    flux_y_hi = (v + v_yn) * (t + t_yn) * 0.25
    flux_y_lo = (v_yp + v) * (t_yp + t) * 0.25
    advect_xy = (flux_x_hi - flux_x_lo) + (flux_y_hi - flux_y_lo)
    carry_through_depth, thermal_spreading_step = depthwise_rate_change(
        t, z_directed_motion, layer_depth_spacing, wall_warmth_bounds
    )
    stacked_layer_count = t_yn - 2.0 * t + t_yp
    current_rate_change = (
        -COURANT * (advect_xy + carry_through_depth)
        + DIFF_Y * stacked_layer_count
        + DIFF_Z * thermal_spreading_step
    )
    linear_system_source = (
        t + NEW_TERM_COEF * current_rate_change + OLD_TERM_COEF * earlier_rate_change
    )
    resulting_warmth_field = periodic_solve(linear_system_source, backward_spread_ratio)
    return (resulting_warmth_field, current_rate_change)


def solution(mesh):
    in_specs = (
        P(None, "gx", "gy"),
        P(None, None, "gx", "gy"),
        P(None, "gx", "gy"),
        P(None, "gx", "gy"),
        P(),
        P(),
        P(None, "gx", "gy"),
    )
    out_specs = (P(None, "gx", "gy"), P(None, "gx", "gy"))
    return jax.shard_map(
        on_device, mesh=mesh, in_specs=in_specs, out_specs=out_specs, check_vma=False
    )
```

```python
import jax
import jax.numpy as jnp
from jax import lax
from jax.sharding import PartitionSpec as P

COURANT = 0.5
DIFF_Y = 0.2
DIFF_Z = 0.25
NEW_TERM_COEF = 0.75
OLD_TERM_COEF = -5.0 / 12.0


def ring_pairs(count, step):
    return [(i, (i + step) % count) for i in range(count)]


def exchange_edges(first, last, axis):
    count = lax.axis_size(axis)
    from_prev = lax.ppermute(last, axis, ring_pairs(count, 1))
    from_next = lax.ppermute(first, axis, ring_pairs(count, -1))
    return from_prev, from_next


def shifted(a, halo, axis, step):
    n = a.shape[axis]
    halo = jnp.expand_dims(halo, axis)
    if step > 0:
        return jnp.concatenate([lax.slice_in_dim(a, 1, n, axis=axis), halo], axis)
    return jnp.concatenate([halo, lax.slice_in_dim(a, 0, n - 1, axis=axis)], axis)


def depthwise_rate_change(
    initial_warmth_field, z_directed_motion, layer_depth_spacing, wall_warmth_bounds
):
    inner_face_transport = (
        (z_directed_motion[:-1] + z_directed_motion[1:])
        * (initial_warmth_field[:-1] + initial_warmth_field[1:])
        * 0.25
    )
    empty_layer_sheet = jnp.zeros_like(initial_warmth_field[:1])
    flux_up = jnp.concatenate([empty_layer_sheet, inner_face_transport, empty_layer_sheet], 0)
    spacing = layer_depth_spacing[:, None, None]
    carry_through_depth = (flux_up[1:] - flux_up[:-1]) / spacing
    warmth_with_ghosts = jnp.concatenate(
        [wall_warmth_bounds[:1], initial_warmth_field, wall_warmth_bounds[1:]], 0
    )
    midway_average = jnp.concatenate(
        [
            layer_depth_spacing[:1],
            0.5 * (layer_depth_spacing[:-1] + layer_depth_spacing[1:]),
            layer_depth_spacing[-1:],
        ],
        0,
    )
    gradient_at_faces = (warmth_with_ghosts[1:] - warmth_with_ghosts[:-1]) / midway_average[
        :, None, None
    ]
    thermal_spreading_step = (gradient_at_faces[1:] - gradient_at_faces[:-1]) / spacing
    return (carry_through_depth, thermal_spreading_step)


def periodic_solve(source, ratio):
    levels, rows, cols = source.shape
    parts = lax.axis_size("gx")
    me = lax.axis_index("gx")
    root = jnp.sqrt(1.0 + 4.0 * ratio)
    mu = (1.0 + root) / ((1.0 + 2.0 * ratio) + root)
    log_lam = jnp.log1p(-mu)[:, None]

    idx = jnp.arange(rows, dtype=jnp.float32)
    dist = jnp.abs(idx[:, None] - idx[None, :])
    kernel = jnp.concatenate(
        [
            jnp.exp(log_lam[:, :, None] * dist[None]),
            jnp.exp(log_lam * (rows - 1 - idx)[None, :])[:, None, :],
            jnp.exp(log_lam * idx[None, :])[:, None, :],
            jnp.zeros((levels, 6, rows), jnp.float32),
        ],
        axis=1,
    )
    product = jnp.einsum(
        "kij,kjc->kic", kernel, source, precision=lax.Precision.HIGHEST
    )
    local = product[:, :rows]
    ends = jnp.transpose(product[:, rows : rows + 2], (1, 0, 2))
    gathered = lax.all_to_all(
        jnp.broadcast_to(ends[None], (parts,) + ends.shape), "gx", 0, 0, tiled=True
    )

    others = jnp.arange(parts)
    whole = -jnp.expm1(log_lam * (parts * rows))
    lag_f = ((me - others - 1) % parts).astype(jnp.float32) * rows
    lag_b = ((others - me - 1) % parts).astype(jnp.float32) * rows
    weight_f = jnp.exp(log_lam * lag_f[None, :]) / whole
    weight_b = jnp.exp(log_lam * lag_b[None, :]) / whole
    carry_f = jnp.sum(weight_f.T[:, :, None] * gathered[:, 0], axis=0)
    carry_b = jnp.sum(weight_b.T[:, :, None] * gathered[:, 1], axis=0)
    into_f = jnp.exp(log_lam * (idx + 1.0)[None, :])
    into_b = jnp.exp(log_lam * (rows - idx)[None, :])
    total = (
        local
        + into_f[:, :, None] * carry_f[:, None, :]
        + into_b[:, :, None] * carry_b[:, None, :]
    )
    return total / root[:, None, None]


def on_device(
    initial_warmth_field,
    horizontal_motion_pair,
    z_directed_motion,
    earlier_rate_change,
    layer_depth_spacing,
    backward_spread_ratio,
    wall_warmth_bounds,
):
    t = initial_warmth_field
    u = horizontal_motion_pair[0]
    v = horizontal_motion_pair[1]
    x_prev, x_next = exchange_edges(
        jnp.stack([t[:, 0, :], u[:, 0, :]]), jnp.stack([t[:, -1, :], u[:, -1, :]]), "gx"
    )
    y_prev, y_next = exchange_edges(
        jnp.stack([t[:, :, 0], v[:, :, 0]]), jnp.stack([t[:, :, -1], v[:, :, -1]]), "gy"
    )
    t_xn = shifted(t, x_next[0], 1, 1)
    t_xp = shifted(t, x_prev[0], 1, -1)
    u_xn = shifted(u, x_next[1], 1, 1)
    u_xp = shifted(u, x_prev[1], 1, -1)
    t_yn = shifted(t, y_next[0], 2, 1)
    t_yp = shifted(t, y_prev[0], 2, -1)
    v_yn = shifted(v, y_next[1], 2, 1)
    v_yp = shifted(v, y_prev[1], 2, -1)

    flux_x_hi = (u + u_xn) * (t + t_xn) * 0.25
    flux_x_lo = (u_xp + u) * (t_xp + t) * 0.25
    flux_y_hi = (v + v_yn) * (t + t_yn) * 0.25
    flux_y_lo = (v_yp + v) * (t_yp + t) * 0.25
    advect_xy = (flux_x_hi - flux_x_lo) + (flux_y_hi - flux_y_lo)
    carry_through_depth, thermal_spreading_step = depthwise_rate_change(
        t, z_directed_motion, layer_depth_spacing, wall_warmth_bounds
    )
    stacked_layer_count = t_yn - 2.0 * t + t_yp
    current_rate_change = (
        -COURANT * (advect_xy + carry_through_depth)
        + DIFF_Y * stacked_layer_count
        + DIFF_Z * thermal_spreading_step
    )
    linear_system_source = (
        t + NEW_TERM_COEF * current_rate_change + OLD_TERM_COEF * earlier_rate_change
    )
    resulting_warmth_field = periodic_solve(linear_system_source, backward_spread_ratio)
    return (resulting_warmth_field, current_rate_change)


def solution(mesh):
    in_specs = (
        P(None, "gx", "gy"),
        P(None, None, "gx", "gy"),
        P(None, "gx", "gy"),
        P(None, "gx", "gy"),
        P(),
        P(),
        P(None, "gx", "gy"),
    )
    out_specs = (P(None, "gx", "gy"), P(None, "gx", "gy"))
    return jax.shard_map(
        on_device, mesh=mesh, in_specs=in_specs, out_specs=out_specs, check_vma=False
    )
```

```python
import jax
import jax.numpy as jnp
from jax import lax
from jax.experimental import pallas as pl
from jax.experimental.pallas import tpu as pltpu
from jax.sharding import PartitionSpec as P

COURANT = 0.5
DIFF_Y = 0.2
DIFF_Z = 0.25
NEW_TERM_COEF = 0.75
OLD_TERM_COEF = -5.0 / 12.0


def ring_pairs(count, step):
    return [(i, (i + step) % count) for i in range(count)]


def exchange_edges(first, last, axis):
    count = lax.axis_size(axis)
    from_prev = lax.ppermute(last, axis, ring_pairs(count, 1))
    from_next = lax.ppermute(first, axis, ring_pairs(count, -1))
    return from_prev, from_next


def periodic_solve(source, ratio):
    levels, rows, cols = source.shape
    parts = lax.axis_size("gx")
    me = lax.axis_index("gx")
    root = jnp.sqrt(1.0 + 4.0 * ratio)
    mu = (1.0 + root) / ((1.0 + 2.0 * ratio) + root)
    log_lam = jnp.log1p(-mu)[:, None]

    idx = jnp.arange(rows, dtype=jnp.float32)
    dist = jnp.abs(idx[:, None] - idx[None, :])
    kernel = jnp.concatenate(
        [
            jnp.exp(log_lam[:, :, None] * dist[None]),
            jnp.exp(log_lam * (rows - 1 - idx)[None, :])[:, None, :],
            jnp.exp(log_lam * idx[None, :])[:, None, :],
            jnp.zeros((levels, 6, rows), jnp.float32),
        ],
        axis=1,
    )
    product = jnp.einsum(
        "kij,kjc->kic", kernel, source, precision=lax.Precision.HIGHEST
    )
    local = product[:, :rows]
    ends = jnp.transpose(product[:, rows : rows + 2], (1, 0, 2))
    gathered = lax.all_to_all(
        jnp.broadcast_to(ends[None], (parts,) + ends.shape), "gx", 0, 0, tiled=True
    )

    others = jnp.arange(parts)
    whole = -jnp.expm1(log_lam * (parts * rows))
    lag_f = ((me - others - 1) % parts).astype(jnp.float32) * rows
    lag_b = ((others - me - 1) % parts).astype(jnp.float32) * rows
    weight_f = jnp.exp(log_lam * lag_f[None, :]) / whole
    weight_b = jnp.exp(log_lam * lag_b[None, :]) / whole
    carry_f = jnp.sum(weight_f.T[:, :, None] * gathered[:, 0], axis=0)
    carry_b = jnp.sum(weight_b.T[:, :, None] * gathered[:, 1], axis=0)
    into_f = jnp.exp(log_lam * (idx + 1.0)[None, :])
    into_b = jnp.exp(log_lam * (rows - idx)[None, :])
    total = (
        local
        + into_f[:, :, None] * carry_f[:, None, :]
        + into_b[:, :, None] * carry_b[:, None, :]
    )
    return total / root[:, None, None]


def stencil_kernel(
    spacing_ref, between_ref, t_ref, u_ref, v_ref, w_ref, early_ref, wall_ref, xh_ref, yh_ref,
    rate_ref, source_ref,
):
    k = pl.program_id(0)
    top = pl.num_programs(0) - 1
    below = jnp.maximum(k - 1, 0)
    above = jnp.minimum(k + 1, top)
    t = t_ref[k]
    u = u_ref[0, 0]
    v = v_ref[0, 0]
    w = w_ref[k]
    rows, cols = t.shape
    row = lax.broadcasted_iota(jnp.int32, (rows, cols), 0)
    col = lax.broadcasted_iota(jnp.int32, (rows, cols), 1)
    xh = xh_ref[0]
    yh = yh_ref[0].T

    def along_x(a, prev, nxt):
        a_next = jnp.where(row == rows - 1, nxt, pltpu.roll(a, rows - 1, 0))
        a_prev = jnp.where(row == 0, prev, pltpu.roll(a, 1, 0))
        return a_prev, a_next

    def along_y(a, prev, nxt):
        a_next = jnp.where(col == cols - 1, nxt, pltpu.roll(a, cols - 1, 1))
        a_prev = jnp.where(col == 0, prev, pltpu.roll(a, 1, 1))
        return a_prev, a_next

    t_xp, t_xn = along_x(t, xh[0:1], xh[2:3])
    u_xp, u_xn = along_x(u, xh[1:2], xh[3:4])
    t_yp, t_yn = along_y(t, yh[:, 0:1], yh[:, 2:3])
    v_yp, v_yn = along_y(v, yh[:, 1:2], yh[:, 3:4])
    flux_x_hi = (u + u_xn) * (t + t_xn) * 0.25
    flux_x_lo = (u_xp + u) * (t_xp + t) * 0.25
    flux_y_hi = (v + v_yn) * (t + t_yn) * 0.25
    flux_y_lo = (v_yp + v) * (t_yp + t) * 0.25
    advect_xy = (flux_x_hi - flux_x_lo) + (flux_y_hi - flux_y_lo)

    t_up = t_ref[above]
    t_dn = t_ref[below]
    flux_up = jnp.where(k == top, 0.0, (w + w_ref[above]) * (t + t_up) * 0.25)
    flux_dn = jnp.where(k == 0, 0.0, (w_ref[below] + w) * (t_dn + t) * 0.25)
    dz = spacing_ref[k]
    carry_through_depth = (flux_up - flux_dn) / dz
    ghost_up = jnp.where(k == top, wall_ref[1], t_up)
    ghost_dn = jnp.where(k == 0, wall_ref[0], t_dn)
    slope_up = (ghost_up - t) / between_ref[k + 1]
    slope_dn = (t - ghost_dn) / between_ref[k]
    thermal_spreading_step = (slope_up - slope_dn) / dz
    stacked_layer_count = t_yn - 2.0 * t + t_yp
    rate = (
        -COURANT * (advect_xy + carry_through_depth)
        + DIFF_Y * stacked_layer_count
        + DIFF_Z * thermal_spreading_step
    )
    rate_ref[0] = rate
    source_ref[0] = t + NEW_TERM_COEF * rate + OLD_TERM_COEF * early_ref[0]


def on_device(
    initial_warmth_field,
    horizontal_motion_pair,
    z_directed_motion,
    earlier_rate_change,
    layer_depth_spacing,
    backward_spread_ratio,
    wall_warmth_bounds,
):
    t = initial_warmth_field
    levels, rows, cols = t.shape
    u = horizontal_motion_pair[0]
    v = horizontal_motion_pair[1]
    x_prev, x_next = exchange_edges(
        jnp.stack([t[:, 0, :], u[:, 0, :]], 1), jnp.stack([t[:, -1, :], u[:, -1, :]], 1), "gx"
    )
    y_prev, y_next = exchange_edges(
        jnp.stack([t[:, :, 0], v[:, :, 0]], 1), jnp.stack([t[:, :, -1], v[:, :, -1]], 1), "gy"
    )
    pad = jnp.zeros((levels, 4, rows), jnp.float32)
    x_halo = jnp.concatenate([x_prev, x_next, pad], 1)
    y_halo = jnp.concatenate([y_prev, y_next, pad], 1)
    between = jnp.concatenate(
        [
            layer_depth_spacing[:1],
            0.5 * (layer_depth_spacing[:-1] + layer_depth_spacing[1:]),
            layer_depth_spacing[-1:],
        ],
        0,
    )
    whole = lambda shape: pl.BlockSpec(shape, lambda k: (0,) * len(shape))
    level = lambda shape: pl.BlockSpec(shape, lambda k: (k,) + (0,) * (len(shape) - 1))
    smem = pl.BlockSpec(memory_space=pltpu.SMEM)
    current_rate_change, linear_system_source = pl.pallas_call(
        stencil_kernel,
        grid=(levels,),
        in_specs=[
            smem,
            smem,
            whole((levels, rows, cols)),
            pl.BlockSpec((1, 1, rows, cols), lambda k: (0, k, 0, 0)),
            pl.BlockSpec((1, 1, rows, cols), lambda k: (1, k, 0, 0)),
            whole((levels, rows, cols)),
            level((1, rows, cols)),
            whole((2, rows, cols)),
            level((1, 8, cols)),
            level((1, 8, rows)),
        ],
        out_specs=[level((1, rows, cols)), level((1, rows, cols))],
        out_shape=[jax.ShapeDtypeStruct(t.shape, jnp.float32)] * 2,
        cost_estimate=pl.CostEstimate(
            flops=80 * t.size, bytes_accessed=4 * 8 * t.size, transcendentals=0
        ),
    )(
        layer_depth_spacing, between, t, horizontal_motion_pair, horizontal_motion_pair,
        z_directed_motion, earlier_rate_change, wall_warmth_bounds, x_halo, y_halo,
    )
    resulting_warmth_field = periodic_solve(linear_system_source, backward_spread_ratio)
    return (resulting_warmth_field, current_rate_change)


def solution(mesh):
    in_specs = (
        P(None, "gx", "gy"),
        P(None, None, "gx", "gy"),
        P(None, "gx", "gy"),
        P(None, "gx", "gy"),
        P(),
        P(),
        P(None, "gx", "gy"),
    )
    out_specs = (P(None, "gx", "gy"), P(None, "gx", "gy"))
    return jax.shard_map(
        on_device, mesh=mesh, in_specs=in_specs, out_specs=out_specs, check_vma=False
    )
```

```python
import jax
import jax.numpy as jnp
from jax import lax
from jax.experimental import pallas as pl
from jax.experimental.pallas import tpu as pltpu
from jax.sharding import PartitionSpec as P

COURANT = 0.5
DIFF_Y = 0.2
DIFF_Z = 0.25
NEW_TERM_COEF = 0.75
OLD_TERM_COEF = -5.0 / 12.0


def ring_pairs(count, step):
    return [(i, (i + step) % count) for i in range(count)]


def exchange_edges(first, last, axis):
    count = lax.axis_size(axis)
    from_prev = lax.ppermute(last, axis, ring_pairs(count, 1))
    from_next = lax.ppermute(first, axis, ring_pairs(count, -1))
    return from_prev, from_next


def spread_root(ratio):
    root = jnp.sqrt(1.0 + 4.0 * ratio)
    mu = (1.0 + root) / ((1.0 + 2.0 * ratio) + root)
    return jnp.log1p(-mu), root


def periodic_solve(source, ends, log_lam, root):
    levels, rows, cols = source.shape
    parts = lax.axis_size("gx")
    me = lax.axis_index("gx")
    log_lam = log_lam[:, None]
    gathered = lax.all_to_all(
        jnp.broadcast_to(ends[None], (parts,) + ends.shape), "gx", 0, 0, tiled=True
    )
    idx = jnp.arange(rows, dtype=jnp.float32)
    dist = jnp.abs(idx[:, None] - idx[None, :])
    kernel = jnp.exp(log_lam[:, :, None] * dist[None])
    local = lax.optimization_barrier(
        jnp.einsum("kij,kjc->kic", kernel, source, precision=lax.Precision.HIGHEST)
    )

    others = jnp.arange(parts)
    whole = -jnp.expm1(log_lam * (parts * rows))
    lag_f = ((me - others - 1) % parts).astype(jnp.float32) * rows
    lag_b = ((others - me - 1) % parts).astype(jnp.float32) * rows
    weight_f = jnp.exp(log_lam * lag_f[None, :]) / whole
    weight_b = jnp.exp(log_lam * lag_b[None, :]) / whole
    carry_f = jnp.sum(weight_f.T[:, :, None] * gathered[:, 0], axis=0)
    carry_b = jnp.sum(weight_b.T[:, :, None] * gathered[:, 1], axis=0)
    into_f = jnp.exp(log_lam * (idx + 1.0)[None, :])
    into_b = jnp.exp(log_lam * (rows - idx)[None, :])
    total = (
        local
        + into_f[:, :, None] * carry_f[:, None, :]
        + into_b[:, :, None] * carry_b[:, None, :]
    )
    return total / root[:, None, None]


def edge_kernel(t_ref, u_ref, v_ref, x_first_ref, x_last_ref, y_first_ref, y_last_ref):
    levels, rows, cols = t_ref.shape
    for k in range(levels):
        t = t_ref[k]
        u = u_ref[0, k]
        x_first_ref[k, 0:1, :] = t[0:1]
        x_first_ref[k, 1:2, :] = u[0:1]
        x_last_ref[k, 0:1, :] = t[rows - 1 : rows]
        x_last_ref[k, 1:2, :] = u[rows - 1 : rows]
        t_cols = t.T
        v_cols = v_ref[0, k].T
        y_first_ref[k, 0:1, :] = t_cols[0:1]
        y_first_ref[k, 1:2, :] = v_cols[0:1]
        y_last_ref[k, 0:1, :] = t_cols[cols - 1 : cols]
        y_last_ref[k, 1:2, :] = v_cols[cols - 1 : cols]


def stencil_kernel(
    inv_dz_ref, inv_between_ref, log_lam_ref, t_ref, u_ref, v_ref, w_ref, early_ref, wall_ref,
    x_prev_ref, x_next_ref, y_prev_ref, y_next_ref, rate_ref, source_ref, ends_ref,
):
    per_step = rate_ref.shape[0]
    levels, rows, cols = t_ref.shape
    top = levels - 1
    row = lax.broadcasted_iota(jnp.int32, (rows, cols), 0)
    col = lax.broadcasted_iota(jnp.int32, (rows, cols), 1)
    row_f = row.astype(jnp.float32)
    slot = lax.broadcasted_iota(jnp.int32, (8, rows), 0)
    for j in range(per_step):
        k = pl.program_id(0) * per_step + j
        below = jnp.maximum(k - 1, 0)
        above = jnp.minimum(k + 1, top)
        t = t_ref[k]
        u = u_ref[0, j]
        v = v_ref[0, j]
        w = w_ref[k]
        xp = x_prev_ref[j]
        xn = x_next_ref[j]
        yp = y_prev_ref[j]
        yn = y_next_ref[j]
        y_rows = jnp.where(
            slot == 0, yp[0:1],
            jnp.where(slot == 1, yp[1:2], jnp.where(slot == 2, yn[0:1], jnp.where(slot == 3, yn[1:2], 0.0))),
        )
        yh = y_rows.T

        def along_x(a, prev, nxt):
            a_next = jnp.where(row == rows - 1, nxt, pltpu.roll(a, rows - 1, 0))
            a_prev = jnp.where(row == 0, prev, pltpu.roll(a, 1, 0))
            return a_prev, a_next

        def along_y(a, prev, nxt):
            a_next = jnp.where(col == cols - 1, nxt, pltpu.roll(a, cols - 1, 1))
            a_prev = jnp.where(col == 0, prev, pltpu.roll(a, 1, 1))
            return a_prev, a_next

        t_xp, t_xn = along_x(t, xp[0:1], xn[0:1])
        u_xp, u_xn = along_x(u, xp[1:2], xn[1:2])
        t_yp, t_yn = along_y(t, yh[:, 0:1], yh[:, 2:3])
        v_yp, v_yn = along_y(v, yh[:, 1:2], yh[:, 3:4])
        flux_x_hi = (u + u_xn) * (t + t_xn) * 0.25
        flux_x_lo = (u_xp + u) * (t_xp + t) * 0.25
        flux_y_hi = (v + v_yn) * (t + t_yn) * 0.25
        flux_y_lo = (v_yp + v) * (t_yp + t) * 0.25
        advect_xy = (flux_x_hi - flux_x_lo) + (flux_y_hi - flux_y_lo)

        t_up = t_ref[above]
        t_dn = t_ref[below]
        flux_up = jnp.where(k == top, 0.0, (w + w_ref[above]) * (t + t_up) * 0.25)
        flux_dn = jnp.where(k == 0, 0.0, (w_ref[below] + w) * (t_dn + t) * 0.25)
        inv_dz = inv_dz_ref[k]
        carry_through_depth = (flux_up - flux_dn) * inv_dz
        ghost_up = jnp.where(k == top, wall_ref[1], t_up)
        ghost_dn = jnp.where(k == 0, wall_ref[0], t_dn)
        slope_up = (ghost_up - t) * inv_between_ref[k + 1]
        slope_dn = (t - ghost_dn) * inv_between_ref[k]
        thermal_spreading_step = (slope_up - slope_dn) * inv_dz
        stacked_layer_count = t_yn - 2.0 * t + t_yp
        rate = (
            -COURANT * (advect_xy + carry_through_depth)
            + DIFF_Y * stacked_layer_count
            + DIFF_Z * thermal_spreading_step
        )
        source = t + NEW_TERM_COEF * rate + OLD_TERM_COEF * early_ref[j]
        rate_ref[j] = rate
        source_ref[j] = source
        log_lam = log_lam_ref[k]
        to_end = jnp.sum(jnp.exp(log_lam * ((rows - 1.0) - row_f)) * source, axis=0, keepdims=True)
        from_start = jnp.sum(jnp.exp(log_lam * row_f) * source, axis=0, keepdims=True)
        ends_ref[j] = jnp.where(slot == 0, to_end, jnp.where(slot == 1, from_start, 0.0))


def on_device(
    initial_warmth_field,
    horizontal_motion_pair,
    z_directed_motion,
    earlier_rate_change,
    layer_depth_spacing,
    backward_spread_ratio,
    wall_warmth_bounds,
):
    t = initial_warmth_field
    levels, rows, cols = t.shape
    f32 = jnp.float32
    pair = lambda i: pl.BlockSpec((1, levels, rows, cols), lambda g: (i, 0, 0, 0))
    x_first, x_last, y_first, y_last = pl.pallas_call(
        edge_kernel,
        grid=(1,),
        in_specs=[pl.BlockSpec((levels, rows, cols), lambda g: (0, 0, 0)), pair(0), pair(1)],
        out_shape=[
            jax.ShapeDtypeStruct((levels, 2, cols), f32),
            jax.ShapeDtypeStruct((levels, 2, cols), f32),
            jax.ShapeDtypeStruct((levels, 2, rows), f32),
            jax.ShapeDtypeStruct((levels, 2, rows), f32),
        ],
    )(t, horizontal_motion_pair, horizontal_motion_pair)
    x_prev, x_next = exchange_edges(x_first, x_last, "gx")
    y_prev, y_next = exchange_edges(y_first, y_last, "gy")

    between = jnp.concatenate(
        [
            layer_depth_spacing[:1],
            0.5 * (layer_depth_spacing[:-1] + layer_depth_spacing[1:]),
            layer_depth_spacing[-1:],
        ],
        0,
    )
    log_lam, root = spread_root(backward_spread_ratio)
    per_step = 4 if levels % 4 == 0 else 1
    whole = lambda shape: pl.BlockSpec(shape, lambda g: (0,) * len(shape))
    level = lambda shape: pl.BlockSpec(shape, lambda g: (g,) + (0,) * (len(shape) - 1))
    smem = pl.BlockSpec(memory_space=pltpu.SMEM)
    current_rate_change, linear_system_source, ends = pl.pallas_call(
        stencil_kernel,
        grid=(levels // per_step,),
        in_specs=[
            smem,
            smem,
            smem,
            whole((levels, rows, cols)),
            pl.BlockSpec((1, per_step, rows, cols), lambda g: (0, g, 0, 0)),
            pl.BlockSpec((1, per_step, rows, cols), lambda g: (1, g, 0, 0)),
            whole((levels, rows, cols)),
            level((per_step, rows, cols)),
            whole((2, rows, cols)),
            level((per_step, 2, cols)),
            level((per_step, 2, cols)),
            level((per_step, 2, rows)),
            level((per_step, 2, rows)),
        ],
        out_specs=[
            level((per_step, rows, cols)),
            level((per_step, rows, cols)),
            level((per_step, 8, cols)),
        ],
        out_shape=[
            jax.ShapeDtypeStruct(t.shape, f32),
            jax.ShapeDtypeStruct(t.shape, f32),
            jax.ShapeDtypeStruct((levels, 8, cols), f32),
        ],
        cost_estimate=pl.CostEstimate(
            flops=100 * t.size, bytes_accessed=4 * 8 * t.size, transcendentals=2 * t.size
        ),
    )(
        1.0 / layer_depth_spacing, 1.0 / between, log_lam, t, horizontal_motion_pair,
        horizontal_motion_pair, z_directed_motion, earlier_rate_change, wall_warmth_bounds,
        x_prev, x_next, y_prev, y_next,
    )
    resulting_warmth_field = periodic_solve(
        linear_system_source, jnp.transpose(ends[:, 0:2], (1, 0, 2)), log_lam, root
    )
    return (resulting_warmth_field, current_rate_change)


def solution(mesh):
    in_specs = (
        P(None, "gx", "gy"),
        P(None, None, "gx", "gy"),
        P(None, "gx", "gy"),
        P(None, "gx", "gy"),
        P(),
        P(),
        P(None, "gx", "gy"),
    )
    out_specs = (P(None, "gx", "gy"), P(None, "gx", "gy"))
    return jax.shard_map(
        on_device, mesh=mesh, in_specs=in_specs, out_specs=out_specs, check_vma=False
    )
```

```python
import jax
import jax.numpy as jnp
from jax import lax
from jax.experimental import pallas as pl
from jax.experimental.pallas import tpu as pltpu
from jax.sharding import PartitionSpec as P

COURANT = 0.5
DIFF_Y = 0.2
DIFF_Z = 0.25
NEW_TERM_COEF = 0.75
OLD_TERM_COEF = -5.0 / 12.0


def ring_pairs(count, step):
    return [(i, (i + step) % count) for i in range(count)]


def exchange_edges(first, last, axis):
    count = lax.axis_size(axis)
    from_prev = lax.ppermute(last, axis, ring_pairs(count, 1))
    from_next = lax.ppermute(first, axis, ring_pairs(count, -1))
    return from_prev, from_next


def spread_root(ratio):
    root = jnp.sqrt(1.0 + 4.0 * ratio)
    mu = (1.0 + root) / ((1.0 + 2.0 * ratio) + root)
    return jnp.log1p(-mu), root


def periodic_solve(source, ends, log_lam, root):
    levels, rows, cols = source.shape
    parts = lax.axis_size("gx")
    me = lax.axis_index("gx")
    log_lam = log_lam[:, None]
    gathered = lax.all_to_all(ends, "gx", 0, 0, tiled=True)
    idx = jnp.arange(rows, dtype=jnp.float32)
    dist = jnp.abs(idx[:, None] - idx[None, :])
    kernel = jnp.exp(log_lam[:, :, None] * dist[None])
    local = lax.optimization_barrier(
        jnp.einsum("kij,kjc->kic", kernel, source, precision=lax.Precision.HIGHEST)
    )

    others = jnp.arange(parts)
    whole = -jnp.expm1(log_lam * (parts * rows))
    lag_f = ((me - others - 1) % parts).astype(jnp.float32) * rows
    lag_b = ((others - me - 1) % parts).astype(jnp.float32) * rows
    weight_f = jnp.exp(log_lam * lag_f[None, :]) / whole
    weight_b = jnp.exp(log_lam * lag_b[None, :]) / whole
    carry_f = jnp.sum(weight_f.T[:, :, None] * gathered[:, :, 0], axis=0)
    carry_b = jnp.sum(weight_b.T[:, :, None] * gathered[:, :, 1], axis=0)
    into_f = jnp.exp(log_lam * (idx + 1.0)[None, :])
    into_b = jnp.exp(log_lam * (rows - idx)[None, :])
    total = (
        local
        + into_f[:, :, None] * carry_f[:, None, :]
        + into_b[:, :, None] * carry_b[:, None, :]
    )
    return total / root[:, None, None]


def edge_kernel(t_ref, u_lo_ref, u_hi_ref, v_ref, x_first_ref, x_last_ref, y_first_ref, y_last_ref):
    per_step, rows, cols = t_ref.shape
    tile = u_lo_ref.shape[2]
    for j in range(per_step):
        t = t_ref[j]
        x_first_ref[j, 0:1, :] = t[0:1]
        x_first_ref[j, 1:2, :] = u_lo_ref[0, j, 0:1, :]
        x_last_ref[j, 0:1, :] = t[rows - 1 : rows]
        x_last_ref[j, 1:2, :] = u_hi_ref[0, j, tile - 1 : tile, :]
        t_cols = t.T
        v_cols = v_ref[0, j].T
        y_first_ref[j, 0:1, :] = t_cols[0:1]
        y_first_ref[j, 1:2, :] = v_cols[0:1]
        y_last_ref[j, 0:1, :] = t_cols[cols - 1 : cols]
        y_last_ref[j, 1:2, :] = v_cols[cols - 1 : cols]


def stencil_kernel(
    inverse_ref, log_lam_ref, t_ref, u_ref, v_ref, w_ref, early_ref, wall_ref,
    x_prev_ref, x_next_ref, y_prev_ref, y_next_ref, rate_ref, source_ref, ends_ref,
):
    per_step = rate_ref.shape[0]
    levels, rows, cols = t_ref.shape
    top = levels - 1
    row = lax.broadcasted_iota(jnp.int32, (rows, cols), 0)
    col = lax.broadcasted_iota(jnp.int32, (rows, cols), 1)
    row_f = row.astype(jnp.float32)
    slot = lax.broadcasted_iota(jnp.int32, (8, rows), 0)
    for j in range(per_step):
        k = pl.program_id(0) * per_step + j
        below = jnp.maximum(k - 1, 0)
        above = jnp.minimum(k + 1, top)
        t = t_ref[k]
        u = u_ref[0, j]
        v = v_ref[0, j]
        w = w_ref[k]
        xp = x_prev_ref[j]
        xn = x_next_ref[j]
        yp = y_prev_ref[j]
        yn = y_next_ref[j]
        y_rows = jnp.where(
            slot == 0, yp[0:1],
            jnp.where(slot == 1, yp[1:2], jnp.where(slot == 2, yn[0:1], jnp.where(slot == 3, yn[1:2], 0.0))),
        )
        yh = y_rows.T

        def along_x(a, prev, nxt):
            a_next = jnp.where(row == rows - 1, nxt, pltpu.roll(a, rows - 1, 0))
            a_prev = jnp.where(row == 0, prev, pltpu.roll(a, 1, 0))
            return a_prev, a_next

        def along_y(a, prev, nxt):
            a_next = jnp.where(col == cols - 1, nxt, pltpu.roll(a, cols - 1, 1))
            a_prev = jnp.where(col == 0, prev, pltpu.roll(a, 1, 1))
            return a_prev, a_next

        t_xp, t_xn = along_x(t, xp[0:1], xn[0:1])
        u_xp, u_xn = along_x(u, xp[1:2], xn[1:2])
        t_yp, t_yn = along_y(t, yh[:, 0:1], yh[:, 2:3])
        v_yp, v_yn = along_y(v, yh[:, 1:2], yh[:, 3:4])
        flux_x_hi = (u + u_xn) * (t + t_xn) * 0.25
        flux_x_lo = (u_xp + u) * (t_xp + t) * 0.25
        flux_y_hi = (v + v_yn) * (t + t_yn) * 0.25
        flux_y_lo = (v_yp + v) * (t_yp + t) * 0.25
        advect_xy = (flux_x_hi - flux_x_lo) + (flux_y_hi - flux_y_lo)

        t_up = t_ref[above]
        t_dn = t_ref[below]
        flux_up = jnp.where(k == top, 0.0, (w + w_ref[above]) * (t + t_up) * 0.25)
        flux_dn = jnp.where(k == 0, 0.0, (w_ref[below] + w) * (t_dn + t) * 0.25)
        inv_dz = inverse_ref[k]
        carry_through_depth = (flux_up - flux_dn) * inv_dz
        ghost_up = jnp.where(k == top, wall_ref[1], t_up)
        ghost_dn = jnp.where(k == 0, wall_ref[0], t_dn)
        slope_up = (ghost_up - t) * inverse_ref[levels + k + 1]
        slope_dn = (t - ghost_dn) * inverse_ref[levels + k]
        thermal_spreading_step = (slope_up - slope_dn) * inv_dz
        stacked_layer_count = t_yn - 2.0 * t + t_yp
        rate = (
            -COURANT * (advect_xy + carry_through_depth)
            + DIFF_Y * stacked_layer_count
            + DIFF_Z * thermal_spreading_step
        )
        source = t + NEW_TERM_COEF * rate + OLD_TERM_COEF * early_ref[j]
        rate_ref[j] = rate
        source_ref[j] = source
        log_lam = log_lam_ref[k]
        to_end = jnp.sum(jnp.exp(log_lam * ((rows - 1.0) - row_f)) * source, axis=0, keepdims=True)
        from_start = jnp.sum(jnp.exp(log_lam * row_f) * source, axis=0, keepdims=True)
        copies = ends_ref.shape[0]
        ends_ref[:, j, 0:1, :] = jnp.broadcast_to(to_end[None], (copies, 1, cols))
        ends_ref[:, j, 1:2, :] = jnp.broadcast_to(from_start[None], (copies, 1, cols))


def on_device(
    initial_warmth_field,
    horizontal_motion_pair,
    z_directed_motion,
    earlier_rate_change,
    layer_depth_spacing,
    backward_spread_ratio,
    wall_warmth_bounds,
):
    t = initial_warmth_field
    levels, rows, cols = t.shape
    f32 = jnp.float32
    per_step = 4 if levels % 4 == 0 else 1
    tile = 8
    level = lambda shape: pl.BlockSpec(shape, lambda g: (g,) + (0,) * (len(shape) - 1))
    x_first, x_last, y_first, y_last = pl.pallas_call(
        edge_kernel,
        grid=(levels // per_step,),
        in_specs=[
            level((per_step, rows, cols)),
            pl.BlockSpec((1, per_step, tile, cols), lambda g: (0, g, 0, 0)),
            pl.BlockSpec((1, per_step, tile, cols), lambda g: (0, g, rows // tile - 1, 0)),
            pl.BlockSpec((1, per_step, rows, cols), lambda g: (1, g, 0, 0)),
        ],
        out_specs=[level((per_step, 2, cols))] * 2 + [level((per_step, 2, rows))] * 2,
        out_shape=[
            jax.ShapeDtypeStruct((levels, 2, cols), f32),
            jax.ShapeDtypeStruct((levels, 2, cols), f32),
            jax.ShapeDtypeStruct((levels, 2, rows), f32),
            jax.ShapeDtypeStruct((levels, 2, rows), f32),
        ],
    )(t, horizontal_motion_pair, horizontal_motion_pair, horizontal_motion_pair)
    x_prev, x_next = exchange_edges(x_first, x_last, "gx")
    y_prev, y_next = exchange_edges(y_first, y_last, "gy")

    between = jnp.concatenate(
        [
            layer_depth_spacing[:1],
            0.5 * (layer_depth_spacing[:-1] + layer_depth_spacing[1:]),
            layer_depth_spacing[-1:],
        ],
        0,
    )
    log_lam, root = spread_root(backward_spread_ratio)
    inverse = 1.0 / jnp.concatenate([layer_depth_spacing, between])
    whole = lambda shape: pl.BlockSpec(shape, lambda g: (0,) * len(shape))
    parts = lax.axis_size("gx")
    smem = pl.BlockSpec(memory_space=pltpu.SMEM)
    current_rate_change, linear_system_source, ends = pl.pallas_call(
        stencil_kernel,
        grid=(levels // per_step,),
        in_specs=[
            smem,
            smem,
            whole((levels, rows, cols)),
            pl.BlockSpec((1, per_step, rows, cols), lambda g: (0, g, 0, 0)),
            pl.BlockSpec((1, per_step, rows, cols), lambda g: (1, g, 0, 0)),
            whole((levels, rows, cols)),
            level((per_step, rows, cols)),
            whole((2, rows, cols)),
            level((per_step, 2, cols)),
            level((per_step, 2, cols)),
            level((per_step, 2, rows)),
            level((per_step, 2, rows)),
        ],
        out_specs=[
            level((per_step, rows, cols)),
            level((per_step, rows, cols)),
            pl.BlockSpec((parts, per_step, 2, cols), lambda g: (0, g, 0, 0)),
        ],
        out_shape=[
            jax.ShapeDtypeStruct(t.shape, f32),
            jax.ShapeDtypeStruct(t.shape, f32),
            jax.ShapeDtypeStruct((parts, levels, 2, cols), f32),
        ],
        cost_estimate=pl.CostEstimate(
            flops=100 * t.size, bytes_accessed=4 * 8 * t.size, transcendentals=2 * t.size
        ),
    )(
        inverse, log_lam, t, horizontal_motion_pair,
        horizontal_motion_pair, z_directed_motion, earlier_rate_change, wall_warmth_bounds,
        x_prev, x_next, y_prev, y_next,
    )
    resulting_warmth_field = periodic_solve(linear_system_source, ends, log_lam, root)
    return (resulting_warmth_field, current_rate_change)


def solution(mesh):
    in_specs = (
        P(None, "gx", "gy"),
        P(None, None, "gx", "gy"),
        P(None, "gx", "gy"),
        P(None, "gx", "gy"),
        P(),
        P(),
        P(None, "gx", "gy"),
    )
    out_specs = (P(None, "gx", "gy"), P(None, "gx", "gy"))
    return jax.shard_map(
        on_device, mesh=mesh, in_specs=in_specs, out_specs=out_specs, check_vma=False
    )
```

```python
import jax
import jax.numpy as jnp
from jax import lax
from jax.experimental import pallas as pl
from jax.experimental.pallas import tpu as pltpu
from jax.sharding import PartitionSpec as P

COURANT = 0.5
DIFF_Y = 0.2
DIFF_Z = 0.25
NEW_TERM_COEF = 0.75
OLD_TERM_COEF = -5.0 / 12.0


def ring_pairs(count, step):
    return [(i, (i + step) % count) for i in range(count)]


def exchange_edges(first, last, axis):
    count = lax.axis_size(axis)
    from_prev = lax.ppermute(last, axis, ring_pairs(count, 1))
    from_next = lax.ppermute(first, axis, ring_pairs(count, -1))
    return from_prev, from_next


def spread_root(ratio):
    root = jnp.sqrt(1.0 + 4.0 * ratio)
    mu = (1.0 + root) / ((1.0 + 2.0 * ratio) + root)
    return jnp.log1p(-mu), root


def periodic_solve(source, ends, log_lam, root):
    levels, rows, cols = source.shape
    parts = lax.axis_size("gx")
    me = lax.axis_index("gx")
    log_lam = log_lam[:, None]
    gathered = lax.all_to_all(ends, "gx", 0, 0, tiled=True)
    idx = jnp.arange(rows, dtype=jnp.float32)
    dist = jnp.abs(idx[:, None] - idx[None, :])
    kernel = jnp.exp(log_lam[:, :, None] * dist[None])
    local = lax.optimization_barrier(
        jnp.einsum("kij,kjc->kic", kernel, source, precision=lax.Precision.HIGHEST)
    )

    others = jnp.arange(parts)
    whole = -jnp.expm1(log_lam * (parts * rows))
    lag_f = ((me - others - 1) % parts).astype(jnp.float32) * rows
    lag_b = ((others - me - 1) % parts).astype(jnp.float32) * rows
    weight_f = jnp.exp(log_lam * lag_f[None, :]) / whole
    weight_b = jnp.exp(log_lam * lag_b[None, :]) / whole
    carry_f = jnp.sum(weight_f.T[:, :, None] * gathered[:, :, 0], axis=0)
    carry_b = jnp.sum(weight_b.T[:, :, None] * gathered[:, :, 1], axis=0)
    into_f = jnp.exp(log_lam * (idx + 1.0)[None, :])
    into_b = jnp.exp(log_lam * (rows - idx)[None, :])
    total = (
        local
        + into_f[:, :, None] * carry_f[:, None, :]
        + into_b[:, :, None] * carry_b[:, None, :]
    )
    return total / root[:, None, None]


def edge_kernel(t_ref, u_lo_ref, u_hi_ref, v_ref, x_first_ref, x_last_ref, y_first_ref, y_last_ref):
    per_step, rows, cols = t_ref.shape
    tile = u_lo_ref.shape[2]
    for j in range(per_step):
        t = t_ref[j]
        x_first_ref[j, 0:1, :] = t[0:1]
        x_first_ref[j, 1:2, :] = u_lo_ref[0, j, 0:1, :]
        x_last_ref[j, 0:1, :] = t[rows - 1 : rows]
        x_last_ref[j, 1:2, :] = u_hi_ref[0, j, tile - 1 : tile, :]
        t_cols = t.T
        v_cols = v_ref[0, j].T
        y_first_ref[j, 0:1, :] = t_cols[0:1]
        y_first_ref[j, 1:2, :] = v_cols[0:1]
        y_last_ref[j, 0:1, :] = t_cols[cols - 1 : cols]
        y_last_ref[j, 1:2, :] = v_cols[cols - 1 : cols]


def stencil_kernel(
    spacing_ref, ratio_ref, t_ref, u_ref, v_ref, w_ref, early_ref, wall_ref,
    x_prev_ref, x_next_ref, y_prev_ref, y_next_ref, rate_ref, source_ref, ends_ref,
):
    per_step = rate_ref.shape[0]
    levels, rows, cols = t_ref.shape
    top = levels - 1
    row = lax.broadcasted_iota(jnp.int32, (rows, cols), 0)
    col = lax.broadcasted_iota(jnp.int32, (rows, cols), 1)
    row_f = row.astype(jnp.float32)
    slot = lax.broadcasted_iota(jnp.int32, (8, rows), 0)
    for j in range(per_step):
        k = pl.program_id(0) * per_step + j
        below = jnp.maximum(k - 1, 0)
        above = jnp.minimum(k + 1, top)
        t = t_ref[k]
        u = u_ref[0, j]
        v = v_ref[0, j]
        w = w_ref[k]
        xp = x_prev_ref[j]
        xn = x_next_ref[j]
        yp = y_prev_ref[j]
        yn = y_next_ref[j]
        y_rows = jnp.where(
            slot == 0, yp[0:1],
            jnp.where(slot == 1, yp[1:2], jnp.where(slot == 2, yn[0:1], jnp.where(slot == 3, yn[1:2], 0.0))),
        )
        yh = y_rows.T

        def along_x(a, prev, nxt):
            a_next = jnp.where(row == rows - 1, nxt, pltpu.roll(a, rows - 1, 0))
            a_prev = jnp.where(row == 0, prev, pltpu.roll(a, 1, 0))
            return a_prev, a_next

        def along_y(a, prev, nxt):
            a_next = jnp.where(col == cols - 1, nxt, pltpu.roll(a, cols - 1, 1))
            a_prev = jnp.where(col == 0, prev, pltpu.roll(a, 1, 1))
            return a_prev, a_next

        t_xp, t_xn = along_x(t, xp[0:1], xn[0:1])
        u_xp, u_xn = along_x(u, xp[1:2], xn[1:2])
        t_yp, t_yn = along_y(t, yh[:, 0:1], yh[:, 2:3])
        v_yp, v_yn = along_y(v, yh[:, 1:2], yh[:, 3:4])
        flux_x_hi = (u + u_xn) * (t + t_xn) * 0.25
        flux_x_lo = (u_xp + u) * (t_xp + t) * 0.25
        flux_y_hi = (v + v_yn) * (t + t_yn) * 0.25
        flux_y_lo = (v_yp + v) * (t_yp + t) * 0.25
        advect_xy = (flux_x_hi - flux_x_lo) + (flux_y_hi - flux_y_lo)

        t_up = t_ref[above]
        t_dn = t_ref[below]
        flux_up = jnp.where(k == top, 0.0, (w + w_ref[above]) * (t + t_up) * 0.25)
        flux_dn = jnp.where(k == 0, 0.0, (w_ref[below] + w) * (t_dn + t) * 0.25)
        dz = spacing_ref[k]
        between_up = jnp.where(k == top, dz, 0.5 * (dz + spacing_ref[above]))
        between_dn = jnp.where(k == 0, dz, 0.5 * (spacing_ref[below] + dz))
        inv_dz = 1.0 / jnp.full((1, cols), dz, jnp.float32)
        carry_through_depth = (flux_up - flux_dn) * inv_dz
        ghost_up = jnp.where(k == top, wall_ref[1], t_up)
        ghost_dn = jnp.where(k == 0, wall_ref[0], t_dn)
        slope_up = (ghost_up - t) * (1.0 / jnp.full((1, cols), between_up, jnp.float32))
        slope_dn = (t - ghost_dn) * (1.0 / jnp.full((1, cols), between_dn, jnp.float32))
        thermal_spreading_step = (slope_up - slope_dn) * inv_dz
        stacked_layer_count = t_yn - 2.0 * t + t_yp
        rate = (
            -COURANT * (advect_xy + carry_through_depth)
            + DIFF_Y * stacked_layer_count
            + DIFF_Z * thermal_spreading_step
        )
        source = t + NEW_TERM_COEF * rate + OLD_TERM_COEF * early_ref[j]
        rate_ref[j] = rate
        source_ref[j] = source
        log_lam = spread_root(jnp.full((1, cols), ratio_ref[k], jnp.float32))[0]
        to_end = jnp.sum(jnp.exp(log_lam * ((rows - 1.0) - row_f)) * source, axis=0, keepdims=True)
        from_start = jnp.sum(jnp.exp(log_lam * row_f) * source, axis=0, keepdims=True)
        copies = ends_ref.shape[0]
        ends_ref[:, j, 0:1, :] = jnp.broadcast_to(to_end[None], (copies, 1, cols))
        ends_ref[:, j, 1:2, :] = jnp.broadcast_to(from_start[None], (copies, 1, cols))


def on_device(
    initial_warmth_field,
    horizontal_motion_pair,
    z_directed_motion,
    earlier_rate_change,
    layer_depth_spacing,
    backward_spread_ratio,
    wall_warmth_bounds,
):
    t = initial_warmth_field
    levels, rows, cols = t.shape
    f32 = jnp.float32
    tile = 8
    whole = lambda shape: pl.BlockSpec(shape, lambda g: (0,) * len(shape))
    x_first, x_last, y_first, y_last = pl.pallas_call(
        edge_kernel,
        grid=(1,),
        in_specs=[
            whole((levels, rows, cols)),
            pl.BlockSpec((1, levels, tile, cols), lambda g: (0, 0, 0, 0)),
            pl.BlockSpec((1, levels, tile, cols), lambda g: (0, 0, rows // tile - 1, 0)),
            pl.BlockSpec((1, levels, rows, cols), lambda g: (1, 0, 0, 0)),
        ],
        out_specs=[whole((levels, 2, cols))] * 2 + [whole((levels, 2, rows))] * 2,
        out_shape=[
            jax.ShapeDtypeStruct((levels, 2, cols), f32),
            jax.ShapeDtypeStruct((levels, 2, cols), f32),
            jax.ShapeDtypeStruct((levels, 2, rows), f32),
            jax.ShapeDtypeStruct((levels, 2, rows), f32),
        ],
    )(t, horizontal_motion_pair, horizontal_motion_pair, horizontal_motion_pair)
    x_prev, x_next = exchange_edges(x_first, x_last, "gx")
    y_prev, y_next = exchange_edges(y_first, y_last, "gy")

    log_lam, root = spread_root(backward_spread_ratio)
    per_step = 4 if levels % 4 == 0 else 1
    level = lambda shape: pl.BlockSpec(shape, lambda g: (g,) + (0,) * (len(shape) - 1))
    parts = lax.axis_size("gx")
    smem = pl.BlockSpec(memory_space=pltpu.SMEM)
    current_rate_change, linear_system_source, ends = pl.pallas_call(
        stencil_kernel,
        grid=(levels // per_step,),
        in_specs=[
            smem,
            smem,
            whole((levels, rows, cols)),
            pl.BlockSpec((1, per_step, rows, cols), lambda g: (0, g, 0, 0)),
            pl.BlockSpec((1, per_step, rows, cols), lambda g: (1, g, 0, 0)),
            whole((levels, rows, cols)),
            level((per_step, rows, cols)),
            whole((2, rows, cols)),
            level((per_step, 2, cols)),
            level((per_step, 2, cols)),
            level((per_step, 2, rows)),
            level((per_step, 2, rows)),
        ],
        out_specs=[
            level((per_step, rows, cols)),
            level((per_step, rows, cols)),
            pl.BlockSpec((parts, per_step, 2, cols), lambda g: (0, g, 0, 0)),
        ],
        out_shape=[
            jax.ShapeDtypeStruct(t.shape, f32),
            jax.ShapeDtypeStruct(t.shape, f32),
            jax.ShapeDtypeStruct((parts, levels, 2, cols), f32),
        ],
        cost_estimate=pl.CostEstimate(
            flops=100 * t.size, bytes_accessed=4 * 8 * t.size, transcendentals=2 * t.size
        ),
    )(
        layer_depth_spacing, backward_spread_ratio, t, horizontal_motion_pair,
        horizontal_motion_pair, z_directed_motion, earlier_rate_change, wall_warmth_bounds,
        x_prev, x_next, y_prev, y_next,
    )
    resulting_warmth_field = periodic_solve(linear_system_source, ends, log_lam, root)
    return (resulting_warmth_field, current_rate_change)


def solution(mesh):
    in_specs = (
        P(None, "gx", "gy"),
        P(None, None, "gx", "gy"),
        P(None, "gx", "gy"),
        P(None, "gx", "gy"),
        P(),
        P(),
        P(None, "gx", "gy"),
    )
    out_specs = (P(None, "gx", "gy"), P(None, "gx", "gy"))
    return jax.shard_map(
        on_device, mesh=mesh, in_specs=in_specs, out_specs=out_specs, check_vma=False
    )
```

```python
import jax
import jax.numpy as jnp
from jax import lax
from jax.experimental import pallas as pl
from jax.experimental.pallas import tpu as pltpu
from jax.sharding import PartitionSpec as P

COURANT = 0.5
DIFF_Y = 0.2
DIFF_Z = 0.25
NEW_TERM_COEF = 0.75
OLD_TERM_COEF = -5.0 / 12.0


def ring_pairs(count, step):
    return [(i, (i + step) % count) for i in range(count)]


def exchange_edges(first, last, axis):
    count = lax.axis_size(axis)
    from_prev = lax.ppermute(last, axis, ring_pairs(count, 1))
    from_next = lax.ppermute(first, axis, ring_pairs(count, -1))
    return from_prev, from_next


def spread_root(ratio):
    root = jnp.sqrt(1.0 + 4.0 * ratio)
    mu = (1.0 + root) / ((1.0 + 2.0 * ratio) + root)
    return jnp.log1p(-mu), root


def periodic_solve(source, ends, log_lam, root):
    levels, rows, cols = source.shape
    parts = lax.axis_size("gx")
    me = lax.axis_index("gx")
    log_lam = log_lam[:, None]
    gathered = lax.all_to_all(ends, "gx", 0, 0, tiled=True)
    idx = jnp.arange(rows, dtype=jnp.float32)
    dist = jnp.abs(idx[:, None] - idx[None, :])
    kernel = jnp.exp(log_lam[:, :, None] * dist[None])
    local = lax.optimization_barrier(
        jnp.einsum("kij,kjc->kic", kernel, source, precision=lax.Precision.HIGHEST)
    )

    others = jnp.arange(parts)
    whole = -jnp.expm1(log_lam * (parts * rows))
    lag_f = ((me - others - 1) % parts).astype(jnp.float32) * rows
    lag_b = ((others - me - 1) % parts).astype(jnp.float32) * rows
    weight_f = jnp.exp(log_lam * lag_f[None, :]) / whole
    weight_b = jnp.exp(log_lam * lag_b[None, :]) / whole
    carry_f = jnp.sum(weight_f.T[:, :, None] * gathered[:, :, 0], axis=0)
    carry_b = jnp.sum(weight_b.T[:, :, None] * gathered[:, :, 1], axis=0)
    into_f = jnp.exp(log_lam * (idx + 1.0)[None, :])
    into_b = jnp.exp(log_lam * (rows - idx)[None, :])
    total = (
        local
        + into_f[:, :, None] * carry_f[:, None, :]
        + into_b[:, :, None] * carry_b[:, None, :]
    )
    return total / root[:, None, None]


def edge_kernel(t_ref, u_lo_ref, u_hi_ref, v_ref, x_first_ref, x_last_ref, y_first_ref, y_last_ref):
    per_step, rows, cols = t_ref.shape
    tile = u_lo_ref.shape[2]
    for j in range(per_step):
        t = t_ref[j]
        x_first_ref[j, 0:1, :] = t[0:1]
        x_first_ref[j, 1:2, :] = u_lo_ref[0, j, 0:1, :]
        x_last_ref[j, 0:1, :] = t[rows - 1 : rows]
        x_last_ref[j, 1:2, :] = u_hi_ref[0, j, tile - 1 : tile, :]
        t_cols = t.T
        v_cols = v_ref[0, j].T
        y_first_ref[j, 0:1, :] = t_cols[0:1]
        y_first_ref[j, 1:2, :] = v_cols[0:1]
        y_last_ref[j, 0:1, :] = t_cols[cols - 1 : cols]
        y_last_ref[j, 1:2, :] = v_cols[cols - 1 : cols]


def stencil_kernel(
    spacing_ref, ratio_ref, t_ref, t_dn_ref, t_up_ref, u_ref, v_ref, w_ref, w_dn_ref, w_up_ref,
    early_ref, wall_ref, x_prev_ref, x_next_ref, y_prev_ref, y_next_ref,
    rate_ref, source_ref, ends_ref,
):
    per_step, rows, cols = t_ref.shape
    top = x_prev_ref.shape[0] - 1
    chunk = 16
    row = lax.broadcasted_iota(jnp.int32, (chunk, cols), 0)
    col = lax.broadcasted_iota(jnp.int32, (chunk, cols), 1)
    row_f = row.astype(jnp.float32)
    slot = lax.broadcasted_iota(jnp.int32, (8, rows), 0)
    copies = ends_ref.shape[0]
    for j in range(per_step):
        k = pl.program_id(0) * per_step + j
        xp = x_prev_ref[k]
        xn = x_next_ref[k]
        yp = y_prev_ref[k]
        yn = y_next_ref[k]
        y_rows = jnp.where(
            slot == 0, yp[0:1],
            jnp.where(slot == 1, yp[1:2], jnp.where(slot == 2, yn[0:1], jnp.where(slot == 3, yn[1:2], 0.0))),
        )
        yh = y_rows.T
        dz = spacing_ref[k]
        dz_up = spacing_ref[jnp.minimum(k + 1, top)]
        dz_dn = spacing_ref[jnp.maximum(k - 1, 0)]
        between_up = jnp.where(k == top, dz, 0.5 * (dz + dz_up))
        between_dn = jnp.where(k == 0, dz, 0.5 * (dz_dn + dz))
        inv_dz = 1.0 / jnp.full((1, cols), dz, jnp.float32)
        inv_up = 1.0 / jnp.full((1, cols), between_up, jnp.float32)
        inv_dn = 1.0 / jnp.full((1, cols), between_dn, jnp.float32)
        log_lam = spread_root(jnp.full((1, cols), ratio_ref[k], jnp.float32))[0]
        t_lvl = t_ref.at[j]
        u_lvl = u_ref.at[0, j]
        w_lvl = w_ref.at[j]
        t_above = t_ref.at[j + 1] if j + 1 < per_step else t_up_ref.at[0]
        w_above = w_ref.at[j + 1] if j + 1 < per_step else w_up_ref.at[0]
        t_below = t_ref.at[j - 1] if j > 0 else t_dn_ref.at[0]
        w_below = w_ref.at[j - 1] if j > 0 else w_dn_ref.at[0]
        to_end = jnp.zeros((1, cols), jnp.float32)
        from_start = jnp.zeros((1, cols), jnp.float32)
        for c in range(rows // chunk):
            lo, hi = c * chunk, (c + 1) * chunk
            t = t_lvl[lo:hi]
            u = u_lvl[lo:hi]
            v = v_ref[0, j, lo:hi]
            w = w_lvl[lo:hi]
            t_prev_row = xp[0:1] if c == 0 else t_lvl[lo - 1 : lo]
            u_prev_row = xp[1:2] if c == 0 else u_lvl[lo - 1 : lo]
            t_next_row = xn[0:1] if hi == rows else t_lvl[hi : hi + 1]
            u_next_row = xn[1:2] if hi == rows else u_lvl[hi : hi + 1]
            t_xn = jnp.where(row == chunk - 1, t_next_row, pltpu.roll(t, chunk - 1, 0))
            t_xp = jnp.where(row == 0, t_prev_row, pltpu.roll(t, 1, 0))
            u_xn = jnp.where(row == chunk - 1, u_next_row, pltpu.roll(u, chunk - 1, 0))
            u_xp = jnp.where(row == 0, u_prev_row, pltpu.roll(u, 1, 0))
            t_yn = jnp.where(col == cols - 1, yh[lo:hi, 2:3], pltpu.roll(t, cols - 1, 1))
            t_yp = jnp.where(col == 0, yh[lo:hi, 0:1], pltpu.roll(t, 1, 1))
            v_yn = jnp.where(col == cols - 1, yh[lo:hi, 3:4], pltpu.roll(v, cols - 1, 1))
            v_yp = jnp.where(col == 0, yh[lo:hi, 1:2], pltpu.roll(v, 1, 1))
            flux_x_hi = (u + u_xn) * (t + t_xn) * 0.25
            flux_x_lo = (u_xp + u) * (t_xp + t) * 0.25
            flux_y_hi = (v + v_yn) * (t + t_yn) * 0.25
            flux_y_lo = (v_yp + v) * (t_yp + t) * 0.25
            advect_xy = (flux_x_hi - flux_x_lo) + (flux_y_hi - flux_y_lo)

            t_up = t_above[lo:hi]
            t_dn = t_below[lo:hi]
            flux_up = (w + w_above[lo:hi]) * (t + t_up) * 0.25
            flux_dn = (w_below[lo:hi] + w) * (t_dn + t) * 0.25
            ghost_up = t_up
            ghost_dn = t_dn
            if j + 1 == per_step:
                flux_up = jnp.where(k == top, 0.0, flux_up)
                ghost_up = jnp.where(k == top, wall_ref[1, lo:hi], t_up)
            if j == 0:
                flux_dn = jnp.where(k == 0, 0.0, flux_dn)
                ghost_dn = jnp.where(k == 0, wall_ref[0, lo:hi], t_dn)
            carry_through_depth = (flux_up - flux_dn) * inv_dz
            slope_up = (ghost_up - t) * inv_up
            slope_dn = (t - ghost_dn) * inv_dn
            thermal_spreading_step = (slope_up - slope_dn) * inv_dz
            stacked_layer_count = t_yn - 2.0 * t + t_yp
            rate = (
                -COURANT * (advect_xy + carry_through_depth)
                + DIFF_Y * stacked_layer_count
                + DIFF_Z * thermal_spreading_step
            )
            source = t + NEW_TERM_COEF * rate + OLD_TERM_COEF * early_ref[j, lo:hi]
            rate_ref[j, lo:hi] = rate
            source_ref[j, lo:hi] = source
            place = row_f + float(lo)
            to_end = to_end + jnp.sum(
                jnp.exp(log_lam * ((rows - 1.0) - place)) * source, axis=0, keepdims=True
            )
            from_start = from_start + jnp.sum(
                jnp.exp(log_lam * place) * source, axis=0, keepdims=True
            )
        ends_ref[:, j, 0:1, :] = jnp.broadcast_to(to_end[None], (copies, 1, cols))
        ends_ref[:, j, 1:2, :] = jnp.broadcast_to(from_start[None], (copies, 1, cols))


def on_device(
    initial_warmth_field,
    horizontal_motion_pair,
    z_directed_motion,
    earlier_rate_change,
    layer_depth_spacing,
    backward_spread_ratio,
    wall_warmth_bounds,
):
    t = initial_warmth_field
    levels, rows, cols = t.shape
    f32 = jnp.float32
    tile = 8
    whole = lambda shape: pl.BlockSpec(shape, lambda g: (0,) * len(shape))
    x_first, x_last, y_first, y_last = pl.pallas_call(
        edge_kernel,
        grid=(1,),
        in_specs=[
            whole((levels, rows, cols)),
            pl.BlockSpec((1, levels, tile, cols), lambda g: (0, 0, 0, 0)),
            pl.BlockSpec((1, levels, tile, cols), lambda g: (0, 0, rows // tile - 1, 0)),
            pl.BlockSpec((1, levels, rows, cols), lambda g: (1, 0, 0, 0)),
        ],
        out_specs=[whole((levels, 2, cols))] * 2 + [whole((levels, 2, rows))] * 2,
        out_shape=[
            jax.ShapeDtypeStruct((levels, 2, cols), f32),
            jax.ShapeDtypeStruct((levels, 2, cols), f32),
            jax.ShapeDtypeStruct((levels, 2, rows), f32),
            jax.ShapeDtypeStruct((levels, 2, rows), f32),
        ],
    )(t, horizontal_motion_pair, horizontal_motion_pair, horizontal_motion_pair)
    x_prev, x_next = exchange_edges(x_first, x_last, "gx")
    y_prev, y_next = exchange_edges(y_first, y_last, "gy")

    log_lam, root = spread_root(backward_spread_ratio)
    per_step = 4 if levels % 4 == 0 else 1
    level = lambda shape: pl.BlockSpec(shape, lambda g: (g,) + (0,) * (len(shape) - 1))
    parts = lax.axis_size("gx")
    vmem = pl.BlockSpec(memory_space=pltpu.VMEM)
    below = pl.BlockSpec(
        (1, rows, cols), lambda g: (jnp.maximum(g * per_step - 1, 0), 0, 0)
    )
    above = pl.BlockSpec(
        (1, rows, cols), lambda g: (jnp.minimum(g * per_step + per_step, levels - 1), 0, 0)
    )
    smem = pl.BlockSpec(memory_space=pltpu.SMEM)
    current_rate_change, linear_system_source, ends = pl.pallas_call(
        stencil_kernel,
        grid=(levels // per_step,),
        in_specs=[
            smem,
            smem,
            level((per_step, rows, cols)),
            below,
            above,
            pl.BlockSpec((1, per_step, rows, cols), lambda g: (0, g, 0, 0)),
            pl.BlockSpec((1, per_step, rows, cols), lambda g: (1, g, 0, 0)),
            level((per_step, rows, cols)),
            below,
            above,
            level((per_step, rows, cols)),
            whole((2, rows, cols)),
            vmem,
            vmem,
            vmem,
            vmem,
        ],
        out_specs=[
            level((per_step, rows, cols)),
            level((per_step, rows, cols)),
            pl.BlockSpec((parts, per_step, 2, cols), lambda g: (0, g, 0, 0)),
        ],
        out_shape=[
            jax.ShapeDtypeStruct(t.shape, f32),
            jax.ShapeDtypeStruct(t.shape, f32),
            jax.ShapeDtypeStruct((parts, levels, 2, cols), f32),
        ],
        cost_estimate=pl.CostEstimate(
            flops=100 * t.size, bytes_accessed=4 * 8 * t.size, transcendentals=2 * t.size
        ),
    )(
        layer_depth_spacing, backward_spread_ratio, t, t, t, horizontal_motion_pair,
        horizontal_motion_pair, z_directed_motion, z_directed_motion, z_directed_motion,
        earlier_rate_change, wall_warmth_bounds,
        x_prev, x_next, y_prev, y_next,
    )
    resulting_warmth_field = periodic_solve(linear_system_source, ends, log_lam, root)
    return (resulting_warmth_field, current_rate_change)


def solution(mesh):
    in_specs = (
        P(None, "gx", "gy"),
        P(None, None, "gx", "gy"),
        P(None, "gx", "gy"),
        P(None, "gx", "gy"),
        P(),
        P(),
        P(None, "gx", "gy"),
    )
    out_specs = (P(None, "gx", "gy"), P(None, "gx", "gy"))
    return jax.shard_map(
        on_device, mesh=mesh, in_specs=in_specs, out_specs=out_specs, check_vma=False
    )
```

```python
import jax
import jax.numpy as jnp
from jax import lax
from jax.experimental import pallas as pl
from jax.experimental.pallas import tpu as pltpu
from jax.sharding import PartitionSpec as P

COURANT = 0.5
DIFF_Y = 0.2
DIFF_Z = 0.25
NEW_TERM_COEF = 0.75
OLD_TERM_COEF = -5.0 / 12.0


def ring_pairs(count, step):
    return [(i, (i + step) % count) for i in range(count)]


def exchange_edges(first, last, axis):
    count = lax.axis_size(axis)
    from_prev = lax.ppermute(last, axis, ring_pairs(count, 1))
    from_next = lax.ppermute(first, axis, ring_pairs(count, -1))
    return from_prev, from_next


def spread_root(ratio):
    root = jnp.sqrt(1.0 + 4.0 * ratio)
    mu = (1.0 + root) / ((1.0 + 2.0 * ratio) + root)
    return jnp.log1p(-mu), root


def periodic_solve(source, ends, log_lam, root):
    levels, rows, cols = source.shape
    parts = lax.axis_size("gx")
    me = lax.axis_index("gx")
    log_lam = log_lam[:, None]
    gathered = lax.all_to_all(ends, "gx", 0, 0, tiled=True)
    idx = jnp.arange(rows, dtype=jnp.float32)
    dist = jnp.abs(idx[:, None] - idx[None, :])
    kernel = jnp.exp(log_lam[:, :, None] * dist[None])
    local = lax.optimization_barrier(
        jnp.einsum("kij,kjc->kic", kernel, source, precision=lax.Precision.HIGHEST)
    )

    others = jnp.arange(parts)
    whole = -jnp.expm1(log_lam * (parts * rows))
    lag_f = ((me - others - 1) % parts).astype(jnp.float32) * rows
    lag_b = ((others - me - 1) % parts).astype(jnp.float32) * rows
    weight_f = jnp.exp(log_lam * lag_f[None, :]) / whole
    weight_b = jnp.exp(log_lam * lag_b[None, :]) / whole
    carry_f = jnp.sum(weight_f.T[:, :, None] * gathered[:, :, 0], axis=0)
    carry_b = jnp.sum(weight_b.T[:, :, None] * gathered[:, :, 1], axis=0)
    into_f = jnp.exp(log_lam * (idx + 1.0)[None, :])
    into_b = jnp.exp(log_lam * (rows - idx)[None, :])
    total = (
        local
        + into_f[:, :, None] * carry_f[:, None, :]
        + into_b[:, :, None] * carry_b[:, None, :]
    )
    return total / root[:, None, None]


def edge_kernel(t_ref, u_lo_ref, u_hi_ref, v_ref, x_first_ref, x_last_ref, y_first_ref, y_last_ref):
    per_step, rows, cols = t_ref.shape
    tile = u_lo_ref.shape[2]
    for j in range(per_step):
        t = t_ref[j]
        x_first_ref[j, 0:1, :] = t[0:1]
        x_first_ref[j, 1:2, :] = u_lo_ref[0, j, 0:1, :]
        x_last_ref[j, 0:1, :] = t[rows - 1 : rows]
        x_last_ref[j, 1:2, :] = u_hi_ref[0, j, tile - 1 : tile, :]
        t_cols = t.T
        v_cols = v_ref[0, j].T
        y_first_ref[j, 0:1, :] = t_cols[0:1]
        y_first_ref[j, 1:2, :] = v_cols[0:1]
        y_last_ref[j, 0:1, :] = t_cols[cols - 1 : cols]
        y_last_ref[j, 1:2, :] = v_cols[cols - 1 : cols]


def stencil_kernel(
    spacing_ref, ratio_ref, t_ref, t_dn_ref, t_up_ref, u_ref, v_ref, w_ref, w_dn_ref, w_up_ref,
    early_ref, wall_ref, x_prev_ref, x_next_ref, y_prev_ref, y_next_ref,
    rate_ref, ends_ref,
):
    per_step, rows, cols = t_ref.shape
    top = x_prev_ref.shape[0] - 1
    chunk = 16
    row = lax.broadcasted_iota(jnp.int32, (chunk, cols), 0)
    col = lax.broadcasted_iota(jnp.int32, (chunk, cols), 1)
    row_f = row.astype(jnp.float32)
    slot = lax.broadcasted_iota(jnp.int32, (8, rows), 0)
    copies = ends_ref.shape[0]
    for j in range(per_step):
        k = pl.program_id(0) * per_step + j
        xp = x_prev_ref[k]
        xn = x_next_ref[k]
        yp = y_prev_ref[k]
        yn = y_next_ref[k]
        y_rows = jnp.where(
            slot == 0, yp[0:1],
            jnp.where(slot == 1, yp[1:2], jnp.where(slot == 2, yn[0:1], jnp.where(slot == 3, yn[1:2], 0.0))),
        )
        yh = y_rows.T
        dz = spacing_ref[k]
        dz_up = spacing_ref[jnp.minimum(k + 1, top)]
        dz_dn = spacing_ref[jnp.maximum(k - 1, 0)]
        between_up = jnp.where(k == top, dz, 0.5 * (dz + dz_up))
        between_dn = jnp.where(k == 0, dz, 0.5 * (dz_dn + dz))
        inv_dz = 1.0 / jnp.full((1, cols), dz, jnp.float32)
        inv_up = 1.0 / jnp.full((1, cols), between_up, jnp.float32)
        inv_dn = 1.0 / jnp.full((1, cols), between_dn, jnp.float32)
        log_lam = spread_root(jnp.full((1, cols), ratio_ref[k], jnp.float32))[0]
        t_lvl = t_ref.at[j]
        u_lvl = u_ref.at[0, j]
        w_lvl = w_ref.at[j]
        t_above = t_ref.at[j + 1] if j + 1 < per_step else t_up_ref.at[0]
        w_above = w_ref.at[j + 1] if j + 1 < per_step else w_up_ref.at[0]
        t_below = t_ref.at[j - 1] if j > 0 else t_dn_ref.at[0]
        w_below = w_ref.at[j - 1] if j > 0 else w_dn_ref.at[0]
        to_end = jnp.zeros((1, cols), jnp.float32)
        from_start = jnp.zeros((1, cols), jnp.float32)
        for c in range(rows // chunk):
            lo, hi = c * chunk, (c + 1) * chunk
            t = t_lvl[lo:hi]
            u = u_lvl[lo:hi]
            v = v_ref[0, j, lo:hi]
            w = w_lvl[lo:hi]
            t_prev_row = xp[0:1] if c == 0 else t_lvl[lo - 1 : lo]
            u_prev_row = xp[1:2] if c == 0 else u_lvl[lo - 1 : lo]
            t_next_row = xn[0:1] if hi == rows else t_lvl[hi : hi + 1]
            u_next_row = xn[1:2] if hi == rows else u_lvl[hi : hi + 1]
            t_xn = jnp.where(row == chunk - 1, t_next_row, pltpu.roll(t, chunk - 1, 0))
            t_xp = jnp.where(row == 0, t_prev_row, pltpu.roll(t, 1, 0))
            u_xn = jnp.where(row == chunk - 1, u_next_row, pltpu.roll(u, chunk - 1, 0))
            u_xp = jnp.where(row == 0, u_prev_row, pltpu.roll(u, 1, 0))
            t_yn = jnp.where(col == cols - 1, yh[lo:hi, 2:3], pltpu.roll(t, cols - 1, 1))
            t_yp = jnp.where(col == 0, yh[lo:hi, 0:1], pltpu.roll(t, 1, 1))
            v_yn = jnp.where(col == cols - 1, yh[lo:hi, 3:4], pltpu.roll(v, cols - 1, 1))
            v_yp = jnp.where(col == 0, yh[lo:hi, 1:2], pltpu.roll(v, 1, 1))
            flux_x_hi = (u + u_xn) * (t + t_xn) * 0.25
            flux_x_lo = (u_xp + u) * (t_xp + t) * 0.25
            flux_y_hi = (v + v_yn) * (t + t_yn) * 0.25
            flux_y_lo = (v_yp + v) * (t_yp + t) * 0.25
            advect_xy = (flux_x_hi - flux_x_lo) + (flux_y_hi - flux_y_lo)

            t_up = t_above[lo:hi]
            t_dn = t_below[lo:hi]
            flux_up = (w + w_above[lo:hi]) * (t + t_up) * 0.25
            flux_dn = (w_below[lo:hi] + w) * (t_dn + t) * 0.25
            ghost_up = t_up
            ghost_dn = t_dn
            if j + 1 == per_step:
                flux_up = jnp.where(k == top, 0.0, flux_up)
                ghost_up = jnp.where(k == top, wall_ref[1, lo:hi], t_up)
            if j == 0:
                flux_dn = jnp.where(k == 0, 0.0, flux_dn)
                ghost_dn = jnp.where(k == 0, wall_ref[0, lo:hi], t_dn)
            carry_through_depth = (flux_up - flux_dn) * inv_dz
            slope_up = (ghost_up - t) * inv_up
            slope_dn = (t - ghost_dn) * inv_dn
            thermal_spreading_step = (slope_up - slope_dn) * inv_dz
            stacked_layer_count = t_yn - 2.0 * t + t_yp
            rate = (
                -COURANT * (advect_xy + carry_through_depth)
                + DIFF_Y * stacked_layer_count
                + DIFF_Z * thermal_spreading_step
            )
            source = t + NEW_TERM_COEF * rate + OLD_TERM_COEF * early_ref[j, lo:hi]
            rate_ref[j, lo:hi] = rate
            place = row_f + float(lo)
            to_end = to_end + jnp.sum(
                jnp.exp(log_lam * ((rows - 1.0) - place)) * source, axis=0, keepdims=True
            )
            from_start = from_start + jnp.sum(
                jnp.exp(log_lam * place) * source, axis=0, keepdims=True
            )
        ends_ref[:, j, 0:1, :] = jnp.broadcast_to(to_end[None], (copies, 1, cols))
        ends_ref[:, j, 1:2, :] = jnp.broadcast_to(from_start[None], (copies, 1, cols))


def on_device(
    initial_warmth_field,
    horizontal_motion_pair,
    z_directed_motion,
    earlier_rate_change,
    layer_depth_spacing,
    backward_spread_ratio,
    wall_warmth_bounds,
):
    t = initial_warmth_field
    levels, rows, cols = t.shape
    f32 = jnp.float32
    tile = 8
    whole = lambda shape: pl.BlockSpec(shape, lambda g: (0,) * len(shape))
    x_first, x_last, y_first, y_last = pl.pallas_call(
        edge_kernel,
        grid=(1,),
        in_specs=[
            whole((levels, rows, cols)),
            pl.BlockSpec((1, levels, tile, cols), lambda g: (0, 0, 0, 0)),
            pl.BlockSpec((1, levels, tile, cols), lambda g: (0, 0, rows // tile - 1, 0)),
            pl.BlockSpec((1, levels, rows, cols), lambda g: (1, 0, 0, 0)),
        ],
        out_specs=[whole((levels, 2, cols))] * 2 + [whole((levels, 2, rows))] * 2,
        out_shape=[
            jax.ShapeDtypeStruct((levels, 2, cols), f32),
            jax.ShapeDtypeStruct((levels, 2, cols), f32),
            jax.ShapeDtypeStruct((levels, 2, rows), f32),
            jax.ShapeDtypeStruct((levels, 2, rows), f32),
        ],
    )(t, horizontal_motion_pair, horizontal_motion_pair, horizontal_motion_pair)
    x_prev, x_next = exchange_edges(x_first, x_last, "gx")
    y_prev, y_next = exchange_edges(y_first, y_last, "gy")

    log_lam, root = spread_root(backward_spread_ratio)
    per_step = 4 if levels % 4 == 0 else 1
    level = lambda shape: pl.BlockSpec(shape, lambda g: (g,) + (0,) * (len(shape) - 1))
    parts = lax.axis_size("gx")
    vmem = pl.BlockSpec(memory_space=pltpu.VMEM)
    below = pl.BlockSpec(
        (1, rows, cols), lambda g: (jnp.maximum(g * per_step - 1, 0), 0, 0)
    )
    above = pl.BlockSpec(
        (1, rows, cols), lambda g: (jnp.minimum(g * per_step + per_step, levels - 1), 0, 0)
    )
    smem = pl.BlockSpec(memory_space=pltpu.SMEM)
    current_rate_change, ends = pl.pallas_call(
        stencil_kernel,
        grid=(levels // per_step,),
        in_specs=[
            smem,
            smem,
            level((per_step, rows, cols)),
            below,
            above,
            pl.BlockSpec((1, per_step, rows, cols), lambda g: (0, g, 0, 0)),
            pl.BlockSpec((1, per_step, rows, cols), lambda g: (1, g, 0, 0)),
            level((per_step, rows, cols)),
            below,
            above,
            level((per_step, rows, cols)),
            whole((2, rows, cols)),
            vmem,
            vmem,
            vmem,
            vmem,
        ],
        out_specs=[
            level((per_step, rows, cols)),
            pl.BlockSpec((parts, per_step, 2, cols), lambda g: (0, g, 0, 0)),
        ],
        out_shape=[
            jax.ShapeDtypeStruct(t.shape, f32),
            jax.ShapeDtypeStruct((parts, levels, 2, cols), f32),
        ],
        cost_estimate=pl.CostEstimate(
            flops=100 * t.size, bytes_accessed=4 * 7 * t.size, transcendentals=2 * t.size
        ),
    )(
        layer_depth_spacing, backward_spread_ratio, t, t, t, horizontal_motion_pair,
        horizontal_motion_pair, z_directed_motion, z_directed_motion, z_directed_motion,
        earlier_rate_change, wall_warmth_bounds,
        x_prev, x_next, y_prev, y_next,
    )
    linear_system_source = (
        t + NEW_TERM_COEF * current_rate_change + OLD_TERM_COEF * earlier_rate_change
    )
    resulting_warmth_field = periodic_solve(linear_system_source, ends, log_lam, root)
    return (resulting_warmth_field, current_rate_change)


def solution(mesh):
    in_specs = (
        P(None, "gx", "gy"),
        P(None, None, "gx", "gy"),
        P(None, "gx", "gy"),
        P(None, "gx", "gy"),
        P(),
        P(),
        P(None, "gx", "gy"),
    )
    out_specs = (P(None, "gx", "gy"), P(None, "gx", "gy"))
    return jax.shard_map(
        on_device, mesh=mesh, in_specs=in_specs, out_specs=out_specs, check_vma=False
    )
```

```python
import jax
import jax.numpy as jnp
from jax import lax
from jax.experimental import pallas as pl
from jax.experimental.pallas import tpu as pltpu
from jax.sharding import PartitionSpec as P

COURANT = 0.5
DIFF_Y = 0.2
DIFF_Z = 0.25
NEW_TERM_COEF = 0.75
OLD_TERM_COEF = -5.0 / 12.0


def ring_pairs(count, step):
    return [(i, (i + step) % count) for i in range(count)]


def exchange_edges(first, last, axis):
    count = lax.axis_size(axis)
    from_prev = lax.ppermute(last, axis, ring_pairs(count, 1))
    from_next = lax.ppermute(first, axis, ring_pairs(count, -1))
    return from_prev, from_next


def spread_root(ratio):
    root = jnp.sqrt(1.0 + 4.0 * ratio)
    mu = (1.0 + root) / ((1.0 + 2.0 * ratio) + root)
    return jnp.log1p(-mu), root


def periodic_solve(source, ends, log_lam, root):
    levels, rows, cols = source.shape
    parts = lax.axis_size("gx")
    me = lax.axis_index("gx")
    log_lam = log_lam[:, None]
    gathered = lax.all_to_all(ends, "gx", 0, 0, tiled=True)
    idx = jnp.arange(rows, dtype=jnp.float32)
    dist = jnp.abs(idx[:, None] - idx[None, :])
    kernel = jnp.exp(log_lam[:, :, None] * dist[None])
    local = lax.optimization_barrier(
        jnp.einsum("kij,kjc->kic", kernel, source, precision=lax.Precision.HIGHEST)
    )

    others = jnp.arange(parts)
    whole = -jnp.expm1(log_lam * (parts * rows))
    lag_f = ((me - others - 1) % parts).astype(jnp.float32) * rows
    lag_b = ((others - me - 1) % parts).astype(jnp.float32) * rows
    weight_f = jnp.exp(log_lam * lag_f[None, :]) / whole
    weight_b = jnp.exp(log_lam * lag_b[None, :]) / whole
    carry_f = jnp.sum(weight_f.T[:, :, None] * gathered[:, :, 0], axis=0)
    carry_b = jnp.sum(weight_b.T[:, :, None] * gathered[:, :, 1], axis=0)
    into_f = jnp.exp(log_lam * (idx + 1.0)[None, :])
    into_b = jnp.exp(log_lam * (rows - idx)[None, :])
    total = (
        local
        + into_f[:, :, None] * carry_f[:, None, :]
        + into_b[:, :, None] * carry_b[:, None, :]
    )
    return total / root[:, None, None]


def edge_kernel(t_ref, u_lo_ref, u_hi_ref, v_ref, x_first_ref, x_last_ref, y_first_ref, y_last_ref):
    per_step, rows, cols = t_ref.shape
    tile = u_lo_ref.shape[2]
    for j in range(per_step):
        t = t_ref[j]
        x_first_ref[j, 0:1, :] = t[0:1]
        x_first_ref[j, 1:2, :] = u_lo_ref[0, j, 0:1, :]
        x_last_ref[j, 0:1, :] = t[rows - 1 : rows]
        x_last_ref[j, 1:2, :] = u_hi_ref[0, j, tile - 1 : tile, :]
        t_cols = t.T
        v_cols = v_ref[0, j].T
        y_first_ref[j, 0:1, :] = t_cols[0:1]
        y_first_ref[j, 1:2, :] = v_cols[0:1]
        y_last_ref[j, 0:1, :] = t_cols[cols - 1 : cols]
        y_last_ref[j, 1:2, :] = v_cols[cols - 1 : cols]


def stencil_kernel(
    spacing_ref, ratio_ref, t_ref, t_dn_ref, t_up_ref, u_ref, v_ref, w_ref, w_dn_ref, w_up_ref,
    early_ref, wall_ref, x_prev_ref, x_next_ref, y_prev_ref, y_next_ref,
    rate_ref, source_ref, ends_ref,
):
    per_step, rows, cols = t_ref.shape
    top = x_prev_ref.shape[0] - 1
    chunk = 16
    row = lax.broadcasted_iota(jnp.int32, (chunk, cols), 0)
    col = lax.broadcasted_iota(jnp.int32, (chunk, cols), 1)
    row_f = row.astype(jnp.float32)
    slot = lax.broadcasted_iota(jnp.int32, (8, rows), 0)
    copies = ends_ref.shape[0]
    for j in range(per_step):
        k = pl.program_id(0) * per_step + j
        xp = x_prev_ref[k]
        xn = x_next_ref[k]
        yp = y_prev_ref[k]
        yn = y_next_ref[k]
        y_rows = jnp.where(
            slot == 0, yp[0:1],
            jnp.where(slot == 1, yp[1:2], jnp.where(slot == 2, yn[0:1], jnp.where(slot == 3, yn[1:2], 0.0))),
        )
        yh = y_rows.T
        dz = spacing_ref[k]
        dz_up = spacing_ref[jnp.minimum(k + 1, top)]
        dz_dn = spacing_ref[jnp.maximum(k - 1, 0)]
        between_up = jnp.where(k == top, dz, 0.5 * (dz + dz_up))
        between_dn = jnp.where(k == 0, dz, 0.5 * (dz_dn + dz))
        inv_dz = 1.0 / jnp.full((1, cols), dz, jnp.float32)
        inv_up = 1.0 / jnp.full((1, cols), between_up, jnp.float32)
        inv_dn = 1.0 / jnp.full((1, cols), between_dn, jnp.float32)
        log_lam = spread_root(jnp.full((1, cols), ratio_ref[k], jnp.float32))[0]
        t_lvl = t_ref.at[j]
        u_lvl = u_ref.at[0, j]
        w_lvl = w_ref.at[j]
        t_above = t_ref.at[j + 1] if j + 1 < per_step else t_up_ref.at[0]
        w_above = w_ref.at[j + 1] if j + 1 < per_step else w_up_ref.at[0]
        t_below = t_ref.at[j - 1] if j > 0 else t_dn_ref.at[0]
        w_below = w_ref.at[j - 1] if j > 0 else w_dn_ref.at[0]
        to_end = jnp.zeros((1, cols), jnp.float32)
        from_start = jnp.zeros((1, cols), jnp.float32)
        for c in range(rows // chunk):
            lo, hi = c * chunk, (c + 1) * chunk
            t = t_lvl[lo:hi]
            u = u_lvl[lo:hi]
            v = v_ref[0, j, lo:hi]
            w = w_lvl[lo:hi]
            t_prev_row = xp[0:1] if c == 0 else t_lvl[lo - 1 : lo]
            u_prev_row = xp[1:2] if c == 0 else u_lvl[lo - 1 : lo]
            t_next_row = xn[0:1] if hi == rows else t_lvl[hi : hi + 1]
            u_next_row = xn[1:2] if hi == rows else u_lvl[hi : hi + 1]
            t_xn = jnp.where(row == chunk - 1, t_next_row, pltpu.roll(t, chunk - 1, 0))
            u_xn = jnp.where(row == chunk - 1, u_next_row, pltpu.roll(u, chunk - 1, 0))
            t_yn = jnp.where(col == cols - 1, yh[lo:hi, 2:3], pltpu.roll(t, cols - 1, 1))
            t_yp = jnp.where(col == 0, yh[lo:hi, 0:1], pltpu.roll(t, 1, 1))
            v_yn = jnp.where(col == cols - 1, yh[lo:hi, 3:4], pltpu.roll(v, cols - 1, 1))
            flux_x_hi = (u + u_xn) * (t + t_xn) * 0.25
            face_x = (u_prev_row + u[0:1]) * (t_prev_row + t[0:1]) * 0.25
            flux_x_lo = jnp.where(row == 0, face_x, pltpu.roll(flux_x_hi, 1, 0))
            flux_y_hi = (v + v_yn) * (t + t_yn) * 0.25
            face_y = (yh[lo:hi, 1:2] + v[:, 0:1]) * (yh[lo:hi, 0:1] + t[:, 0:1]) * 0.25
            flux_y_lo = jnp.where(col == 0, face_y, pltpu.roll(flux_y_hi, 1, 1))
            advect_xy = (flux_x_hi - flux_x_lo) + (flux_y_hi - flux_y_lo)

            t_up = t_above[lo:hi]
            t_dn = t_below[lo:hi]
            flux_up = (w + w_above[lo:hi]) * (t + t_up) * 0.25
            flux_dn = (w_below[lo:hi] + w) * (t_dn + t) * 0.25
            ghost_up = t_up
            ghost_dn = t_dn
            if j + 1 == per_step:
                flux_up = jnp.where(k == top, 0.0, flux_up)
                ghost_up = jnp.where(k == top, wall_ref[1, lo:hi], t_up)
            if j == 0:
                flux_dn = jnp.where(k == 0, 0.0, flux_dn)
                ghost_dn = jnp.where(k == 0, wall_ref[0, lo:hi], t_dn)
            carry_through_depth = (flux_up - flux_dn) * inv_dz
            slope_up = (ghost_up - t) * inv_up
            slope_dn = (t - ghost_dn) * inv_dn
            thermal_spreading_step = (slope_up - slope_dn) * inv_dz
            stacked_layer_count = t_yn - 2.0 * t + t_yp
            rate = (
                -COURANT * (advect_xy + carry_through_depth)
                + DIFF_Y * stacked_layer_count
                + DIFF_Z * thermal_spreading_step
            )
            source = t + NEW_TERM_COEF * rate + OLD_TERM_COEF * early_ref[j, lo:hi]
            rate_ref[j, lo:hi] = rate
            source_ref[j, lo:hi] = source
            place = row_f + float(lo)
            to_end = to_end + jnp.sum(
                jnp.exp(log_lam * ((rows - 1.0) - place)) * source, axis=0, keepdims=True
            )
            from_start = from_start + jnp.sum(
                jnp.exp(log_lam * place) * source, axis=0, keepdims=True
            )
        ends_ref[:, j, 0:1, :] = jnp.broadcast_to(to_end[None], (copies, 1, cols))
        ends_ref[:, j, 1:2, :] = jnp.broadcast_to(from_start[None], (copies, 1, cols))


def on_device(
    initial_warmth_field,
    horizontal_motion_pair,
    z_directed_motion,
    earlier_rate_change,
    layer_depth_spacing,
    backward_spread_ratio,
    wall_warmth_bounds,
):
    t = initial_warmth_field
    levels, rows, cols = t.shape
    f32 = jnp.float32
    tile = 8
    whole = lambda shape: pl.BlockSpec(shape, lambda g: (0,) * len(shape))
    x_first, x_last, y_first, y_last = pl.pallas_call(
        edge_kernel,
        grid=(1,),
        in_specs=[
            whole((levels, rows, cols)),
            pl.BlockSpec((1, levels, tile, cols), lambda g: (0, 0, 0, 0)),
            pl.BlockSpec((1, levels, tile, cols), lambda g: (0, 0, rows // tile - 1, 0)),
            pl.BlockSpec((1, levels, rows, cols), lambda g: (1, 0, 0, 0)),
        ],
        out_specs=[whole((levels, 2, cols))] * 2 + [whole((levels, 2, rows))] * 2,
        out_shape=[
            jax.ShapeDtypeStruct((levels, 2, cols), f32),
            jax.ShapeDtypeStruct((levels, 2, cols), f32),
            jax.ShapeDtypeStruct((levels, 2, rows), f32),
            jax.ShapeDtypeStruct((levels, 2, rows), f32),
        ],
    )(t, horizontal_motion_pair, horizontal_motion_pair, horizontal_motion_pair)
    x_prev, x_next = exchange_edges(x_first, x_last, "gx")
    y_prev, y_next = exchange_edges(y_first, y_last, "gy")

    log_lam, root = spread_root(backward_spread_ratio)
    per_step = 4 if levels % 4 == 0 else 1
    level = lambda shape: pl.BlockSpec(shape, lambda g: (g,) + (0,) * (len(shape) - 1))
    parts = lax.axis_size("gx")
    vmem = pl.BlockSpec(memory_space=pltpu.VMEM)
    below = pl.BlockSpec(
        (1, rows, cols), lambda g: (jnp.maximum(g * per_step - 1, 0), 0, 0)
    )
    above = pl.BlockSpec(
        (1, rows, cols), lambda g: (jnp.minimum(g * per_step + per_step, levels - 1), 0, 0)
    )
    smem = pl.BlockSpec(memory_space=pltpu.SMEM)
    current_rate_change, linear_system_source, ends = pl.pallas_call(
        stencil_kernel,
        grid=(levels // per_step,),
        in_specs=[
            smem,
            smem,
            level((per_step, rows, cols)),
            below,
            above,
            pl.BlockSpec((1, per_step, rows, cols), lambda g: (0, g, 0, 0)),
            pl.BlockSpec((1, per_step, rows, cols), lambda g: (1, g, 0, 0)),
            level((per_step, rows, cols)),
            below,
            above,
            level((per_step, rows, cols)),
            whole((2, rows, cols)),
            vmem,
            vmem,
            vmem,
            vmem,
        ],
        out_specs=[
            level((per_step, rows, cols)),
            level((per_step, rows, cols)),
            pl.BlockSpec((parts, per_step, 2, cols), lambda g: (0, g, 0, 0)),
        ],
        out_shape=[
            jax.ShapeDtypeStruct(t.shape, f32),
            jax.ShapeDtypeStruct(t.shape, f32),
            jax.ShapeDtypeStruct((parts, levels, 2, cols), f32),
        ],
        cost_estimate=pl.CostEstimate(
            flops=100 * t.size, bytes_accessed=4 * 8 * t.size, transcendentals=2 * t.size
        ),
    )(
        layer_depth_spacing, backward_spread_ratio, t, t, t, horizontal_motion_pair,
        horizontal_motion_pair, z_directed_motion, z_directed_motion, z_directed_motion,
        earlier_rate_change, wall_warmth_bounds,
        x_prev, x_next, y_prev, y_next,
    )
    resulting_warmth_field = periodic_solve(linear_system_source, ends, log_lam, root)
    return (resulting_warmth_field, current_rate_change)


def solution(mesh):
    in_specs = (
        P(None, "gx", "gy"),
        P(None, None, "gx", "gy"),
        P(None, "gx", "gy"),
        P(None, "gx", "gy"),
        P(),
        P(),
        P(None, "gx", "gy"),
    )
    out_specs = (P(None, "gx", "gy"), P(None, "gx", "gy"))
    return jax.shard_map(
        on_device, mesh=mesh, in_specs=in_specs, out_specs=out_specs, check_vma=False
    )
```

```python
import jax
import jax.numpy as jnp
from jax import lax
from jax.experimental import pallas as pl
from jax.experimental.pallas import tpu as pltpu
from jax.sharding import PartitionSpec as P

COURANT = 0.5
DIFF_Y = 0.2
DIFF_Z = 0.25
NEW_TERM_COEF = 0.75
OLD_TERM_COEF = -5.0 / 12.0


def ring_pairs(count, step):
    return [(i, (i + step) % count) for i in range(count)]


def exchange_edges(first, last, axis):
    count = lax.axis_size(axis)
    from_prev = lax.ppermute(last, axis, ring_pairs(count, 1))
    from_next = lax.ppermute(first, axis, ring_pairs(count, -1))
    return from_prev, from_next


def spread_root(ratio):
    root = jnp.sqrt(1.0 + 4.0 * ratio)
    mu = (1.0 + root) / ((1.0 + 2.0 * ratio) + root)
    return jnp.log1p(-mu), root


def periodic_solve(source, ends, log_lam, root):
    levels, rows, cols = source.shape
    parts = lax.axis_size("gx")
    me = lax.axis_index("gx")
    log_lam = log_lam[:, None]
    gathered = lax.all_to_all(ends, "gx", 0, 0, tiled=True)
    idx = jnp.arange(rows, dtype=jnp.float32)
    dist = jnp.abs(idx[:, None] - idx[None, :])
    kernel = jnp.exp(log_lam[:, :, None] * dist[None])
    local = lax.optimization_barrier(
        jnp.einsum("kij,kjc->kic", kernel, source, precision=lax.Precision.HIGHEST)
    )

    others = jnp.arange(parts)
    whole = -jnp.expm1(log_lam * (parts * rows))
    lag_f = ((me - others - 1) % parts).astype(jnp.float32) * rows
    lag_b = ((others - me - 1) % parts).astype(jnp.float32) * rows
    weight_f = jnp.exp(log_lam * lag_f[None, :]) / whole
    weight_b = jnp.exp(log_lam * lag_b[None, :]) / whole
    carry_f = jnp.sum(weight_f.T[:, :, None] * gathered[:, :, 0], axis=0)
    carry_b = jnp.sum(weight_b.T[:, :, None] * gathered[:, :, 1], axis=0)
    into_f = jnp.exp(log_lam * (idx + 1.0)[None, :])
    into_b = jnp.exp(log_lam * (rows - idx)[None, :])
    total = (
        local
        + into_f[:, :, None] * carry_f[:, None, :]
        + into_b[:, :, None] * carry_b[:, None, :]
    )
    return total / root[:, None, None]


def edge_kernel(t_ref, u_lo_ref, u_hi_ref, v_ref, x_first_ref, x_last_ref, y_first_ref, y_last_ref):
    per_step, rows, cols = t_ref.shape
    tile = u_lo_ref.shape[2]
    for j in range(per_step):
        t = t_ref[j]
        x_first_ref[j, 0:1, :] = t[0:1]
        x_first_ref[j, 1:2, :] = u_lo_ref[0, j, 0:1, :]
        x_last_ref[j, 0:1, :] = t[rows - 1 : rows]
        x_last_ref[j, 1:2, :] = u_hi_ref[0, j, tile - 1 : tile, :]
        t_cols = t.T
        v_cols = v_ref[0, j].T
        y_first_ref[j, 0:1, :] = t_cols[0:1]
        y_first_ref[j, 1:2, :] = v_cols[0:1]
        y_last_ref[j, 0:1, :] = t_cols[cols - 1 : cols]
        y_last_ref[j, 1:2, :] = v_cols[cols - 1 : cols]


def stencil_kernel(
    spacing_ref, ratio_ref, t_ref, t_dn_ref, t_up_ref, u_ref, v_ref, w_ref, w_dn_ref, w_up_ref,
    early_ref, wall_ref, x_prev_ref, x_next_ref, y_prev_ref, y_next_ref,
    rate_ref, source_ref, ends_ref,
):
    per_step, rows, cols = t_ref.shape
    top = x_prev_ref.shape[0] - 1
    chunk = 16
    row = lax.broadcasted_iota(jnp.int32, (chunk, cols), 0)
    col = lax.broadcasted_iota(jnp.int32, (chunk, cols), 1)
    row_f = row.astype(jnp.float32)
    slot = lax.broadcasted_iota(jnp.int32, (8, rows), 0)
    copies = ends_ref.shape[0]
    for j in range(per_step):
        k = pl.program_id(0) * per_step + j
        xp = x_prev_ref[k]
        xn = x_next_ref[k]
        yp = y_prev_ref[k]
        yn = y_next_ref[k]
        y_rows = jnp.where(
            slot == 0, yp[0:1],
            jnp.where(slot == 1, yp[1:2], jnp.where(slot == 2, yn[0:1], jnp.where(slot == 3, yn[1:2], 0.0))),
        )
        yh = y_rows.T
        dz = spacing_ref[k]
        dz_up = spacing_ref[jnp.minimum(k + 1, top)]
        dz_dn = spacing_ref[jnp.maximum(k - 1, 0)]
        between_up = jnp.where(k == top, dz, 0.5 * (dz + dz_up))
        between_dn = jnp.where(k == 0, dz, 0.5 * (dz_dn + dz))
        inv_dz = 1.0 / jnp.full((1, cols), dz, jnp.float32)
        inv_up = 1.0 / jnp.full((1, cols), between_up, jnp.float32)
        inv_dn = 1.0 / jnp.full((1, cols), between_dn, jnp.float32)
        log_lam = spread_root(jnp.full((1, cols), ratio_ref[k], jnp.float32))[0]
        t_lvl = t_ref.at[j]
        u_lvl = u_ref.at[0, j]
        w_lvl = w_ref.at[j]
        t_above = t_ref.at[j + 1] if j + 1 < per_step else t_up_ref.at[0]
        w_above = w_ref.at[j + 1] if j + 1 < per_step else w_up_ref.at[0]
        t_below = t_ref.at[j - 1] if j > 0 else t_dn_ref.at[0]
        w_below = w_ref.at[j - 1] if j > 0 else w_dn_ref.at[0]
        to_end = jnp.zeros((1, cols), jnp.float32)
        from_start = jnp.zeros((1, cols), jnp.float32)
        for c in range(rows // chunk):
            lo, hi = c * chunk, (c + 1) * chunk
            t = t_lvl[lo:hi]
            u = u_lvl[lo:hi]
            v = v_ref[0, j, lo:hi]
            w = w_lvl[lo:hi]
            t_prev_row = xp[0:1] if c == 0 else t_lvl[lo - 1 : lo]
            u_prev_row = xp[1:2] if c == 0 else u_lvl[lo - 1 : lo]
            t_next_row = xn[0:1] if hi == rows else t_lvl[hi : hi + 1]
            u_next_row = xn[1:2] if hi == rows else u_lvl[hi : hi + 1]
            t_xn = jnp.where(row == chunk - 1, t_next_row, pltpu.roll(t, chunk - 1, 0))
            u_xn = jnp.where(row == chunk - 1, u_next_row, pltpu.roll(u, chunk - 1, 0))
            t_yn = jnp.where(col == cols - 1, yh[lo:hi, 2:3], pltpu.roll(t, cols - 1, 1))
            t_yp = jnp.where(col == 0, yh[lo:hi, 0:1], pltpu.roll(t, 1, 1))
            v_yn = jnp.where(col == cols - 1, yh[lo:hi, 3:4], pltpu.roll(v, cols - 1, 1))
            v_yp = jnp.where(col == 0, yh[lo:hi, 1:2], pltpu.roll(v, 1, 1))
            flux_x_hi = (u + u_xn) * (t + t_xn) * 0.25
            face_x = (u_prev_row + u[0:1]) * (t_prev_row + t[0:1]) * 0.25
            flux_x_lo = jnp.where(row == 0, face_x, pltpu.roll(flux_x_hi, 1, 0))
            flux_y_hi = (v + v_yn) * (t + t_yn) * 0.25
            flux_y_lo = (v_yp + v) * (t_yp + t) * 0.25
            advect_xy = (flux_x_hi - flux_x_lo) + (flux_y_hi - flux_y_lo)

            t_up = t_above[lo:hi]
            t_dn = t_below[lo:hi]
            flux_up = (w + w_above[lo:hi]) * (t + t_up) * 0.25
            flux_dn = (w_below[lo:hi] + w) * (t_dn + t) * 0.25
            ghost_up = t_up
            ghost_dn = t_dn
            if j + 1 == per_step:
                flux_up = jnp.where(k == top, 0.0, flux_up)
                ghost_up = jnp.where(k == top, wall_ref[1, lo:hi], t_up)
            if j == 0:
                flux_dn = jnp.where(k == 0, 0.0, flux_dn)
                ghost_dn = jnp.where(k == 0, wall_ref[0, lo:hi], t_dn)
            carry_through_depth = (flux_up - flux_dn) * inv_dz
            slope_up = (ghost_up - t) * inv_up
            slope_dn = (t - ghost_dn) * inv_dn
            thermal_spreading_step = (slope_up - slope_dn) * inv_dz
            stacked_layer_count = t_yn - 2.0 * t + t_yp
            rate = (
                -COURANT * (advect_xy + carry_through_depth)
                + DIFF_Y * stacked_layer_count
                + DIFF_Z * thermal_spreading_step
            )
            source = t + NEW_TERM_COEF * rate + OLD_TERM_COEF * early_ref[j, lo:hi]
            rate_ref[j, lo:hi] = rate
            source_ref[j, lo:hi] = source
            place = row_f + float(lo)
            to_end = to_end + jnp.sum(
                jnp.exp(log_lam * ((rows - 1.0) - place)) * source, axis=0, keepdims=True
            )
            from_start = from_start + jnp.sum(
                jnp.exp(log_lam * place) * source, axis=0, keepdims=True
            )
        ends_ref[:, j, 0:1, :] = jnp.broadcast_to(to_end[None], (copies, 1, cols))
        ends_ref[:, j, 1:2, :] = jnp.broadcast_to(from_start[None], (copies, 1, cols))


def on_device(
    initial_warmth_field,
    horizontal_motion_pair,
    z_directed_motion,
    earlier_rate_change,
    layer_depth_spacing,
    backward_spread_ratio,
    wall_warmth_bounds,
):
    t = initial_warmth_field
    levels, rows, cols = t.shape
    f32 = jnp.float32
    tile = 8
    whole = lambda shape: pl.BlockSpec(shape, lambda g: (0,) * len(shape))
    x_first, x_last, y_first, y_last = pl.pallas_call(
        edge_kernel,
        grid=(1,),
        in_specs=[
            whole((levels, rows, cols)),
            pl.BlockSpec((1, levels, tile, cols), lambda g: (0, 0, 0, 0)),
            pl.BlockSpec((1, levels, tile, cols), lambda g: (0, 0, rows // tile - 1, 0)),
            pl.BlockSpec((1, levels, rows, cols), lambda g: (1, 0, 0, 0)),
        ],
        out_specs=[whole((levels, 2, cols))] * 2 + [whole((levels, 2, rows))] * 2,
        out_shape=[
            jax.ShapeDtypeStruct((levels, 2, cols), f32),
            jax.ShapeDtypeStruct((levels, 2, cols), f32),
            jax.ShapeDtypeStruct((levels, 2, rows), f32),
            jax.ShapeDtypeStruct((levels, 2, rows), f32),
        ],
    )(t, horizontal_motion_pair, horizontal_motion_pair, horizontal_motion_pair)
    x_prev, x_next = exchange_edges(x_first, x_last, "gx")
    y_prev, y_next = exchange_edges(y_first, y_last, "gy")

    log_lam, root = spread_root(backward_spread_ratio)
    per_step = 4 if levels % 4 == 0 else 1
    level = lambda shape: pl.BlockSpec(shape, lambda g: (g,) + (0,) * (len(shape) - 1))
    parts = lax.axis_size("gx")
    vmem = pl.BlockSpec(memory_space=pltpu.VMEM)
    below = pl.BlockSpec(
        (1, rows, cols), lambda g: (jnp.maximum(g * per_step - 1, 0), 0, 0)
    )
    above = pl.BlockSpec(
        (1, rows, cols), lambda g: (jnp.minimum(g * per_step + per_step, levels - 1), 0, 0)
    )
    smem = pl.BlockSpec(memory_space=pltpu.SMEM)
    current_rate_change, linear_system_source, ends = pl.pallas_call(
        stencil_kernel,
        grid=(levels // per_step,),
        in_specs=[
            smem,
            smem,
            level((per_step, rows, cols)),
            below,
            above,
            pl.BlockSpec((1, per_step, rows, cols), lambda g: (0, g, 0, 0)),
            pl.BlockSpec((1, per_step, rows, cols), lambda g: (1, g, 0, 0)),
            level((per_step, rows, cols)),
            below,
            above,
            level((per_step, rows, cols)),
            whole((2, rows, cols)),
            vmem,
            vmem,
            vmem,
            vmem,
        ],
        out_specs=[
            level((per_step, rows, cols)),
            level((per_step, rows, cols)),
            pl.BlockSpec((parts, per_step, 2, cols), lambda g: (0, g, 0, 0)),
        ],
        out_shape=[
            jax.ShapeDtypeStruct(t.shape, f32),
            jax.ShapeDtypeStruct(t.shape, f32),
            jax.ShapeDtypeStruct((parts, levels, 2, cols), f32),
        ],
        cost_estimate=pl.CostEstimate(
            flops=100 * t.size, bytes_accessed=4 * 8 * t.size, transcendentals=2 * t.size
        ),
    )(
        layer_depth_spacing, backward_spread_ratio, t, t, t, horizontal_motion_pair,
        horizontal_motion_pair, z_directed_motion, z_directed_motion, z_directed_motion,
        earlier_rate_change, wall_warmth_bounds,
        x_prev, x_next, y_prev, y_next,
    )
    resulting_warmth_field = periodic_solve(linear_system_source, ends, log_lam, root)
    return (resulting_warmth_field, current_rate_change)


def solution(mesh):
    in_specs = (
        P(None, "gx", "gy"),
        P(None, None, "gx", "gy"),
        P(None, "gx", "gy"),
        P(None, "gx", "gy"),
        P(),
        P(),
        P(None, "gx", "gy"),
    )
    out_specs = (P(None, "gx", "gy"), P(None, "gx", "gy"))
    return jax.shard_map(
        on_device, mesh=mesh, in_specs=in_specs, out_specs=out_specs, check_vma=False
    )
```

```python
import jax
import jax.numpy as jnp
from jax import lax
from jax.experimental import pallas as pl
from jax.experimental.pallas import tpu as pltpu
from jax.sharding import PartitionSpec as P

COURANT = 0.5
DIFF_Y = 0.2
DIFF_Z = 0.25
NEW_TERM_COEF = 0.75
OLD_TERM_COEF = -5.0 / 12.0


def ring_pairs(count, step):
    return [(i, (i + step) % count) for i in range(count)]


def exchange_edges(first, last, axis):
    count = lax.axis_size(axis)
    from_prev = lax.ppermute(last, axis, ring_pairs(count, 1))
    from_next = lax.ppermute(first, axis, ring_pairs(count, -1))
    return from_prev, from_next


def spread_root(ratio):
    root = jnp.sqrt(1.0 + 4.0 * ratio)
    mu = (1.0 + root) / ((1.0 + 2.0 * ratio) + root)
    return jnp.log1p(-mu), root


def periodic_solve(source, ends, log_lam, root):
    levels, rows, cols = source.shape
    parts = lax.axis_size("gx")
    me = lax.axis_index("gx")
    log_lam = log_lam[:, None]
    gathered = lax.all_to_all(ends, "gx", 0, 0, tiled=True)
    idx = jnp.arange(rows, dtype=jnp.float32)
    dist = jnp.abs(idx[:, None] - idx[None, :])
    kernel = jnp.exp(log_lam[:, :, None] * dist[None])
    local = lax.optimization_barrier(
        jnp.einsum("kij,kjc->kic", kernel, source, precision=lax.Precision.HIGHEST)
    )

    others = jnp.arange(parts)
    whole = -jnp.expm1(log_lam * (parts * rows))
    lag_f = ((me - others - 1) % parts).astype(jnp.float32) * rows
    lag_b = ((others - me - 1) % parts).astype(jnp.float32) * rows
    weight_f = jnp.exp(log_lam * lag_f[None, :]) / whole
    weight_b = jnp.exp(log_lam * lag_b[None, :]) / whole
    carry_f = jnp.sum(weight_f.T[:, :, None] * gathered[:, :, 0], axis=0)
    carry_b = jnp.sum(weight_b.T[:, :, None] * gathered[:, :, 1], axis=0)
    into_f = jnp.exp(log_lam * (idx + 1.0)[None, :])
    into_b = jnp.exp(log_lam * (rows - idx)[None, :])
    total = (
        local
        + into_f[:, :, None] * carry_f[:, None, :]
        + into_b[:, :, None] * carry_b[:, None, :]
    )
    return total / root[:, None, None]


def edge_kernel(t_ref, u_lo_ref, u_hi_ref, v_ref, x_first_ref, x_last_ref, y_first_ref, y_last_ref):
    per_step, rows, cols = t_ref.shape
    tile = u_lo_ref.shape[2]
    for j in range(per_step):
        t = t_ref[j]
        x_first_ref[j, 0:1, :] = t[0:1]
        x_first_ref[j, 1:2, :] = u_lo_ref[0, j, 0:1, :]
        x_last_ref[j, 0:1, :] = t[rows - 1 : rows]
        x_last_ref[j, 1:2, :] = u_hi_ref[0, j, tile - 1 : tile, :]
        t_cols = t.T
        v_cols = v_ref[0, j].T
        y_first_ref[j, 0:1, :] = t_cols[0:1]
        y_first_ref[j, 1:2, :] = v_cols[0:1]
        y_last_ref[j, 0:1, :] = t_cols[cols - 1 : cols]
        y_last_ref[j, 1:2, :] = v_cols[cols - 1 : cols]


def stencil_kernel(
    spacing_ref, ratio_ref, t_ref, t_dn_ref, t_up_ref, u_ref, v_ref, w_ref, w_dn_ref, w_up_ref,
    early_ref, wall_ref, x_prev_ref, x_next_ref, y_prev_ref, y_next_ref,
    rate_ref, source_ref, ends_ref,
):
    per_step, rows, cols = t_ref.shape
    top = x_prev_ref.shape[0] - 1
    chunk = 16
    row = lax.broadcasted_iota(jnp.int32, (chunk, cols), 0)
    col = lax.broadcasted_iota(jnp.int32, (chunk, cols), 1)
    row_f = row.astype(jnp.float32)
    slot = lax.broadcasted_iota(jnp.int32, (8, rows), 0)
    copies = ends_ref.shape[0]
    for j in range(per_step):
        k = pl.program_id(0) * per_step + j
        xp = x_prev_ref[k]
        xn = x_next_ref[k]
        yp = y_prev_ref[k]
        yn = y_next_ref[k]
        y_rows = jnp.where(
            slot == 0, yp[0:1],
            jnp.where(slot == 1, yp[1:2], jnp.where(slot == 2, yn[0:1], jnp.where(slot == 3, yn[1:2], 0.0))),
        )
        yh = y_rows.T
        dz = spacing_ref[k]
        dz_up = spacing_ref[jnp.minimum(k + 1, top)]
        dz_dn = spacing_ref[jnp.maximum(k - 1, 0)]
        between_up = jnp.where(k == top, dz, 0.5 * (dz + dz_up))
        between_dn = jnp.where(k == 0, dz, 0.5 * (dz_dn + dz))
        inv_dz = 1.0 / jnp.full((1, cols), dz, jnp.float32)
        inv_up = 1.0 / jnp.full((1, cols), between_up, jnp.float32)
        inv_dn = 1.0 / jnp.full((1, cols), between_dn, jnp.float32)
        log_lam = spread_root(jnp.full((1, cols), ratio_ref[k], jnp.float32))[0]
        t_lvl = t_ref.at[j]
        u_lvl = u_ref.at[0, j]
        w_lvl = w_ref.at[j]
        t_above = t_ref.at[j + 1] if j + 1 < per_step else t_up_ref.at[0]
        w_above = w_ref.at[j + 1] if j + 1 < per_step else w_up_ref.at[0]
        t_below = t_ref.at[j - 1] if j > 0 else t_dn_ref.at[0]
        w_below = w_ref.at[j - 1] if j > 0 else w_dn_ref.at[0]
        to_end = jnp.zeros((1, cols), jnp.float32)
        from_start = jnp.zeros((1, cols), jnp.float32)
        for c in range(rows // chunk):
            lo, hi = c * chunk, (c + 1) * chunk
            t = t_lvl[lo:hi]
            u = u_lvl[lo:hi]
            v = v_ref[0, j, lo:hi]
            w = w_lvl[lo:hi]
            t_prev_row = xp[0:1] if c == 0 else t_lvl[lo - 1 : lo]
            u_prev_row = xp[1:2] if c == 0 else u_lvl[lo - 1 : lo]
            t_next_row = xn[0:1] if hi == rows else t_lvl[hi : hi + 1]
            u_next_row = xn[1:2] if hi == rows else u_lvl[hi : hi + 1]
            t_xn = jnp.where(row == chunk - 1, t_next_row, pltpu.roll(t, chunk - 1, 0))
            t_xp = jnp.where(row == 0, t_prev_row, pltpu.roll(t, 1, 0))
            u_xn = jnp.where(row == chunk - 1, u_next_row, pltpu.roll(u, chunk - 1, 0))
            u_xp = jnp.where(row == 0, u_prev_row, pltpu.roll(u, 1, 0))
            t_yn = jnp.where(col == cols - 1, yh[lo:hi, 2:3], pltpu.roll(t, cols - 1, 1))
            t_yp = jnp.where(col == 0, yh[lo:hi, 0:1], pltpu.roll(t, 1, 1))
            v_yn = jnp.where(col == cols - 1, yh[lo:hi, 3:4], pltpu.roll(v, cols - 1, 1))
            v_yp = jnp.where(col == 0, yh[lo:hi, 1:2], pltpu.roll(v, 1, 1))
            flux_x_hi = (u + u_xn) * (t + t_xn) * 0.25
            flux_x_lo = (u_xp + u) * (t_xp + t) * 0.25
            flux_y_hi = (v + v_yn) * (t + t_yn) * 0.25
            flux_y_lo = (v_yp + v) * (t_yp + t) * 0.25
            advect_xy = (flux_x_hi - flux_x_lo) + (flux_y_hi - flux_y_lo)

            t_up = t_above[lo:hi]
            t_dn = t_below[lo:hi]
            flux_up = (w + w_above[lo:hi]) * (t + t_up) * 0.25
            flux_dn = (w_below[lo:hi] + w) * (t_dn + t) * 0.25
            ghost_up = t_up
            ghost_dn = t_dn
            if j + 1 == per_step:
                flux_up = jnp.where(k == top, 0.0, flux_up)
                ghost_up = jnp.where(k == top, wall_ref[1, lo:hi], t_up)
            if j == 0:
                flux_dn = jnp.where(k == 0, 0.0, flux_dn)
                ghost_dn = jnp.where(k == 0, wall_ref[0, lo:hi], t_dn)
            carry_through_depth = (flux_up - flux_dn) * inv_dz
            slope_up = (ghost_up - t) * inv_up
            slope_dn = (t - ghost_dn) * inv_dn
            thermal_spreading_step = (slope_up - slope_dn) * inv_dz
            stacked_layer_count = t_yn - 2.0 * t + t_yp
            rate = (
                -COURANT * (advect_xy + carry_through_depth)
                + DIFF_Y * stacked_layer_count
                + DIFF_Z * thermal_spreading_step
            )
            source = t + NEW_TERM_COEF * rate + OLD_TERM_COEF * early_ref[j, lo:hi]
            rate_ref[j, lo:hi] = rate
            source_ref[j, lo:hi] = source
            place = row_f + float(lo)
            to_end = to_end + jnp.sum(
                jnp.exp(log_lam * ((rows - 1.0) - place)) * source, axis=0, keepdims=True
            )
            from_start = from_start + jnp.sum(
                jnp.exp(log_lam * place) * source, axis=0, keepdims=True
            )
        ends_ref[:, j, 0:1, :] = jnp.broadcast_to(to_end[None], (copies, 1, cols))
        ends_ref[:, j, 1:2, :] = jnp.broadcast_to(from_start[None], (copies, 1, cols))


def on_device(
    initial_warmth_field,
    horizontal_motion_pair,
    z_directed_motion,
    earlier_rate_change,
    layer_depth_spacing,
    backward_spread_ratio,
    wall_warmth_bounds,
):
    t = initial_warmth_field
    levels, rows, cols = t.shape
    f32 = jnp.float32
    tile = 8
    whole = lambda shape: pl.BlockSpec(shape, lambda g: (0,) * len(shape))
    x_first, x_last, y_first, y_last = pl.pallas_call(
        edge_kernel,
        grid=(1,),
        in_specs=[
            whole((levels, rows, cols)),
            pl.BlockSpec((1, levels, tile, cols), lambda g: (0, 0, 0, 0)),
            pl.BlockSpec((1, levels, tile, cols), lambda g: (0, 0, rows // tile - 1, 0)),
            pl.BlockSpec((1, levels, rows, cols), lambda g: (1, 0, 0, 0)),
        ],
        out_specs=[whole((levels, 2, cols))] * 2 + [whole((levels, 2, rows))] * 2,
        out_shape=[
            jax.ShapeDtypeStruct((levels, 2, cols), f32),
            jax.ShapeDtypeStruct((levels, 2, cols), f32),
            jax.ShapeDtypeStruct((levels, 2, rows), f32),
            jax.ShapeDtypeStruct((levels, 2, rows), f32),
        ],
    )(t, horizontal_motion_pair, horizontal_motion_pair, horizontal_motion_pair)
    x_prev, x_next = exchange_edges(x_first, x_last, "gx")
    y_prev, y_next = exchange_edges(y_first, y_last, "gy")

    log_lam, root = spread_root(backward_spread_ratio)
    per_step = 8 if levels % 8 == 0 else 1
    level = lambda shape: pl.BlockSpec(shape, lambda g: (g,) + (0,) * (len(shape) - 1))
    parts = lax.axis_size("gx")
    vmem = pl.BlockSpec(memory_space=pltpu.VMEM)
    below = pl.BlockSpec(
        (1, rows, cols), lambda g: (jnp.maximum(g * per_step - 1, 0), 0, 0)
    )
    above = pl.BlockSpec(
        (1, rows, cols), lambda g: (jnp.minimum(g * per_step + per_step, levels - 1), 0, 0)
    )
    smem = pl.BlockSpec(memory_space=pltpu.SMEM)
    current_rate_change, linear_system_source, ends = pl.pallas_call(
        stencil_kernel,
        grid=(levels // per_step,),
        in_specs=[
            smem,
            smem,
            level((per_step, rows, cols)),
            below,
            above,
            pl.BlockSpec((1, per_step, rows, cols), lambda g: (0, g, 0, 0)),
            pl.BlockSpec((1, per_step, rows, cols), lambda g: (1, g, 0, 0)),
            level((per_step, rows, cols)),
            below,
            above,
            level((per_step, rows, cols)),
            whole((2, rows, cols)),
            vmem,
            vmem,
            vmem,
            vmem,
        ],
        out_specs=[
            level((per_step, rows, cols)),
            level((per_step, rows, cols)),
            pl.BlockSpec((parts, per_step, 2, cols), lambda g: (0, g, 0, 0)),
        ],
        out_shape=[
            jax.ShapeDtypeStruct(t.shape, f32),
            jax.ShapeDtypeStruct(t.shape, f32),
            jax.ShapeDtypeStruct((parts, levels, 2, cols), f32),
        ],
        cost_estimate=pl.CostEstimate(
            flops=100 * t.size, bytes_accessed=4 * 8 * t.size, transcendentals=2 * t.size
        ),
    )(
        layer_depth_spacing, backward_spread_ratio, t, t, t, horizontal_motion_pair,
        horizontal_motion_pair, z_directed_motion, z_directed_motion, z_directed_motion,
        earlier_rate_change, wall_warmth_bounds,
        x_prev, x_next, y_prev, y_next,
    )
    resulting_warmth_field = periodic_solve(linear_system_source, ends, log_lam, root)
    return (resulting_warmth_field, current_rate_change)


def solution(mesh):
    in_specs = (
        P(None, "gx", "gy"),
        P(None, None, "gx", "gy"),
        P(None, "gx", "gy"),
        P(None, "gx", "gy"),
        P(),
        P(),
        P(None, "gx", "gy"),
    )
    out_specs = (P(None, "gx", "gy"), P(None, "gx", "gy"))
    return jax.shard_map(
        on_device, mesh=mesh, in_specs=in_specs, out_specs=out_specs, check_vma=False
    )
```

```python
import jax
import jax.numpy as jnp
from jax import lax
from jax.experimental import pallas as pl
from jax.experimental.pallas import tpu as pltpu
from jax.sharding import PartitionSpec as P

COURANT = 0.5
DIFF_Y = 0.2
DIFF_Z = 0.25
NEW_TERM_COEF = 0.75
OLD_TERM_COEF = -5.0 / 12.0


def ring_pairs(count, step):
    return [(i, (i + step) % count) for i in range(count)]


def exchange_edges(first, last, axis):
    count = lax.axis_size(axis)
    from_prev = lax.ppermute(last, axis, ring_pairs(count, 1))
    from_next = lax.ppermute(first, axis, ring_pairs(count, -1))
    return from_prev, from_next


def spread_root(ratio):
    root = jnp.sqrt(1.0 + 4.0 * ratio)
    mu = (1.0 + root) / ((1.0 + 2.0 * ratio) + root)
    return jnp.log1p(-mu), root


def periodic_solve(source, ends, log_lam, root):
    levels, rows, cols = source.shape
    parts = lax.axis_size("gx")
    me = lax.axis_index("gx")
    log_lam = log_lam[:, None]
    gathered = lax.all_to_all(ends, "gx", 0, 0, tiled=True)
    idx = jnp.arange(rows, dtype=jnp.float32)
    dist = jnp.abs(idx[:, None] - idx[None, :])
    kernel = jnp.exp(log_lam[:, :, None] * dist[None])
    local = lax.optimization_barrier(
        jnp.einsum("kij,kjc->kic", kernel, source, precision=lax.Precision.HIGHEST)
    )

    others = jnp.arange(parts)
    whole = -jnp.expm1(log_lam * (parts * rows))
    lag_f = ((me - others - 1) % parts).astype(jnp.float32) * rows
    lag_b = ((others - me - 1) % parts).astype(jnp.float32) * rows
    weight_f = jnp.exp(log_lam * lag_f[None, :]) / whole
    weight_b = jnp.exp(log_lam * lag_b[None, :]) / whole
    carry_f = jnp.sum(weight_f.T[:, :, None] * gathered[:, :, 0], axis=0)
    carry_b = jnp.sum(weight_b.T[:, :, None] * gathered[:, :, 1], axis=0)
    into_f = jnp.exp(log_lam * (idx + 1.0)[None, :])
    into_b = jnp.exp(log_lam * (rows - idx)[None, :])
    total = (
        local
        + into_f[:, :, None] * carry_f[:, None, :]
        + into_b[:, :, None] * carry_b[:, None, :]
    )
    return total / root[:, None, None]


def edge_kernel(t_ref, u_lo_ref, u_hi_ref, v_ref, x_first_ref, x_last_ref, y_first_ref, y_last_ref):
    per_step, rows, cols = t_ref.shape
    tile = u_lo_ref.shape[2]
    for j in range(per_step):
        t = t_ref[j]
        x_first_ref[j, 0:1, :] = t[0:1]
        x_first_ref[j, 1:2, :] = u_lo_ref[0, j, 0:1, :]
        x_last_ref[j, 0:1, :] = t[rows - 1 : rows]
        x_last_ref[j, 1:2, :] = u_hi_ref[0, j, tile - 1 : tile, :]
        t_cols = t.T
        v_cols = v_ref[0, j].T
        y_first_ref[j, 0:1, :] = t_cols[0:1]
        y_first_ref[j, 1:2, :] = v_cols[0:1]
        y_last_ref[j, 0:1, :] = t_cols[cols - 1 : cols]
        y_last_ref[j, 1:2, :] = v_cols[cols - 1 : cols]


def stencil_kernel(
    spacing_ref, ratio_ref, t_ref, t_dn_ref, t_up_ref, u_ref, v_ref, w_ref, w_dn_ref, w_up_ref,
    early_ref, wall_ref, x_prev_ref, x_next_ref, y_prev_ref, y_next_ref,
    rate_ref, source_ref, ends_ref,
):
    per_step, rows, cols = t_ref.shape
    top = x_prev_ref.shape[0] - 1
    chunk = 16
    row = lax.broadcasted_iota(jnp.int32, (chunk, cols), 0)
    col = lax.broadcasted_iota(jnp.int32, (chunk, cols), 1)
    row_f = row.astype(jnp.float32)
    slot = lax.broadcasted_iota(jnp.int32, (8, rows), 0)
    copies = ends_ref.shape[0]
    for j in range(per_step):
        k = pl.program_id(0) * per_step + j
        xp = x_prev_ref[k]
        xn = x_next_ref[k]
        yp = y_prev_ref[k]
        yn = y_next_ref[k]
        y_rows = jnp.where(
            slot == 0, yp[0:1],
            jnp.where(slot == 1, yp[1:2], jnp.where(slot == 2, yn[0:1], jnp.where(slot == 3, yn[1:2], 0.0))),
        )
        yh = y_rows.T
        dz = spacing_ref[k]
        dz_up = spacing_ref[jnp.minimum(k + 1, top)]
        dz_dn = spacing_ref[jnp.maximum(k - 1, 0)]
        between_up = jnp.where(k == top, dz, 0.5 * (dz + dz_up))
        between_dn = jnp.where(k == 0, dz, 0.5 * (dz_dn + dz))
        inv_dz = 1.0 / jnp.full((1, cols), dz, jnp.float32)
        inv_up = 1.0 / jnp.full((1, cols), between_up, jnp.float32)
        inv_dn = 1.0 / jnp.full((1, cols), between_dn, jnp.float32)
        log_lam = spread_root(jnp.full((1, cols), ratio_ref[k], jnp.float32))[0]
        t_lvl = t_ref.at[j]
        u_lvl = u_ref.at[0, j]
        w_lvl = w_ref.at[j]
        t_above = t_ref.at[j + 1] if j + 1 < per_step else t_up_ref.at[0]
        w_above = w_ref.at[j + 1] if j + 1 < per_step else w_up_ref.at[0]
        t_below = t_ref.at[j - 1] if j > 0 else t_dn_ref.at[0]
        w_below = w_ref.at[j - 1] if j > 0 else w_dn_ref.at[0]
        to_end = jnp.zeros((1, cols), jnp.float32)
        from_start = jnp.zeros((1, cols), jnp.float32)
        for c in range(rows // chunk):
            lo, hi = c * chunk, (c + 1) * chunk
            t = t_lvl[lo:hi]
            u = u_lvl[lo:hi]
            v = v_ref[0, j, lo:hi]
            w = w_lvl[lo:hi]
            t_prev_row = xp[0:1] if c == 0 else t_lvl[lo - 1 : lo]
            u_prev_row = xp[1:2] if c == 0 else u_lvl[lo - 1 : lo]
            t_next_row = xn[0:1] if hi == rows else t_lvl[hi : hi + 1]
            u_next_row = xn[1:2] if hi == rows else u_lvl[hi : hi + 1]
            t_xn = jnp.where(row == chunk - 1, t_next_row, pltpu.roll(t, chunk - 1, 0))
            t_xp = jnp.where(row == 0, t_prev_row, pltpu.roll(t, 1, 0))
            u_xn = jnp.where(row == chunk - 1, u_next_row, pltpu.roll(u, chunk - 1, 0))
            u_xp = jnp.where(row == 0, u_prev_row, pltpu.roll(u, 1, 0))
            t_yn = jnp.where(col == cols - 1, yh[lo:hi, 2:3], pltpu.roll(t, cols - 1, 1))
            t_yp = jnp.where(col == 0, yh[lo:hi, 0:1], pltpu.roll(t, 1, 1))
            v_yn = jnp.where(col == cols - 1, yh[lo:hi, 3:4], pltpu.roll(v, cols - 1, 1))
            v_yp = jnp.where(col == 0, yh[lo:hi, 1:2], pltpu.roll(v, 1, 1))
            flux_x_hi = (u + u_xn) * (t + t_xn) * 0.25
            flux_x_lo = (u_xp + u) * (t_xp + t) * 0.25
            flux_y_hi = (v + v_yn) * (t + t_yn) * 0.25
            flux_y_lo = (v_yp + v) * (t_yp + t) * 0.25
            advect_xy = (flux_x_hi - flux_x_lo) + (flux_y_hi - flux_y_lo)

            t_up = t_above[lo:hi]
            t_dn = t_below[lo:hi]
            flux_up = (w + w_above[lo:hi]) * (t + t_up) * 0.25
            flux_dn = (w_below[lo:hi] + w) * (t_dn + t) * 0.25
            ghost_up = t_up
            ghost_dn = t_dn
            if j + 1 == per_step:
                flux_up = jnp.where(k == top, 0.0, flux_up)
                ghost_up = jnp.where(k == top, wall_ref[1, lo:hi], t_up)
            if j == 0:
                flux_dn = jnp.where(k == 0, 0.0, flux_dn)
                ghost_dn = jnp.where(k == 0, wall_ref[0, lo:hi], t_dn)
            carry_through_depth = (flux_up - flux_dn) * inv_dz
            slope_up = (ghost_up - t) * inv_up
            slope_dn = (t - ghost_dn) * inv_dn
            thermal_spreading_step = (slope_up - slope_dn) * inv_dz
            stacked_layer_count = t_yn - 2.0 * t + t_yp
            rate = (
                -COURANT * (advect_xy + carry_through_depth)
                + DIFF_Y * stacked_layer_count
                + DIFF_Z * thermal_spreading_step
            )
            source = t + NEW_TERM_COEF * rate + OLD_TERM_COEF * early_ref[j, lo:hi]
            rate_ref[j, lo:hi] = rate
            source_ref[j, lo:hi] = source
            place = row_f + float(lo)
            to_end = to_end + jnp.sum(
                jnp.exp(log_lam * ((rows - 1.0) - place)) * source, axis=0, keepdims=True
            )
            from_start = from_start + jnp.sum(
                jnp.exp(log_lam * place) * source, axis=0, keepdims=True
            )
        ends_ref[:, j, 0:1, :] = jnp.broadcast_to(to_end[None], (copies, 1, cols))
        ends_ref[:, j, 1:2, :] = jnp.broadcast_to(from_start[None], (copies, 1, cols))


def on_device(
    initial_warmth_field,
    horizontal_motion_pair,
    z_directed_motion,
    earlier_rate_change,
    layer_depth_spacing,
    backward_spread_ratio,
    wall_warmth_bounds,
):
    t = initial_warmth_field
    levels, rows, cols = t.shape
    f32 = jnp.float32
    tile = 8
    whole = lambda shape: pl.BlockSpec(shape, lambda g: (0,) * len(shape))
    x_first, x_last, y_first, y_last = pl.pallas_call(
        edge_kernel,
        grid=(1,),
        in_specs=[
            whole((levels, rows, cols)),
            pl.BlockSpec((1, levels, tile, cols), lambda g: (0, 0, 0, 0)),
            pl.BlockSpec((1, levels, tile, cols), lambda g: (0, 0, rows // tile - 1, 0)),
            pl.BlockSpec((1, levels, rows, cols), lambda g: (1, 0, 0, 0)),
        ],
        out_specs=[whole((levels, 2, cols))] * 2 + [whole((levels, 2, rows))] * 2,
        out_shape=[
            jax.ShapeDtypeStruct((levels, 2, cols), f32),
            jax.ShapeDtypeStruct((levels, 2, cols), f32),
            jax.ShapeDtypeStruct((levels, 2, rows), f32),
            jax.ShapeDtypeStruct((levels, 2, rows), f32),
        ],
    )(t, horizontal_motion_pair, horizontal_motion_pair, horizontal_motion_pair)
    x_prev, x_next = exchange_edges(x_first, x_last, "gx")
    y_prev, y_next = exchange_edges(y_first, y_last, "gy")

    log_lam, root = spread_root(backward_spread_ratio)
    per_step = 2 if levels % 2 == 0 else 1
    level = lambda shape: pl.BlockSpec(shape, lambda g: (g,) + (0,) * (len(shape) - 1))
    parts = lax.axis_size("gx")
    vmem = pl.BlockSpec(memory_space=pltpu.VMEM)
    below = pl.BlockSpec(
        (1, rows, cols), lambda g: (jnp.maximum(g * per_step - 1, 0), 0, 0)
    )
    above = pl.BlockSpec(
        (1, rows, cols), lambda g: (jnp.minimum(g * per_step + per_step, levels - 1), 0, 0)
    )
    smem = pl.BlockSpec(memory_space=pltpu.SMEM)
    current_rate_change, linear_system_source, ends = pl.pallas_call(
        stencil_kernel,
        grid=(levels // per_step,),
        in_specs=[
            smem,
            smem,
            level((per_step, rows, cols)),
            below,
            above,
            pl.BlockSpec((1, per_step, rows, cols), lambda g: (0, g, 0, 0)),
            pl.BlockSpec((1, per_step, rows, cols), lambda g: (1, g, 0, 0)),
            level((per_step, rows, cols)),
            below,
            above,
            level((per_step, rows, cols)),
            whole((2, rows, cols)),
            vmem,
            vmem,
            vmem,
            vmem,
        ],
        out_specs=[
            level((per_step, rows, cols)),
            level((per_step, rows, cols)),
            pl.BlockSpec((parts, per_step, 2, cols), lambda g: (0, g, 0, 0)),
        ],
        out_shape=[
            jax.ShapeDtypeStruct(t.shape, f32),
            jax.ShapeDtypeStruct(t.shape, f32),
            jax.ShapeDtypeStruct((parts, levels, 2, cols), f32),
        ],
        cost_estimate=pl.CostEstimate(
            flops=100 * t.size, bytes_accessed=4 * 8 * t.size, transcendentals=2 * t.size
        ),
    )(
        layer_depth_spacing, backward_spread_ratio, t, t, t, horizontal_motion_pair,
        horizontal_motion_pair, z_directed_motion, z_directed_motion, z_directed_motion,
        earlier_rate_change, wall_warmth_bounds,
        x_prev, x_next, y_prev, y_next,
    )
    resulting_warmth_field = periodic_solve(linear_system_source, ends, log_lam, root)
    return (resulting_warmth_field, current_rate_change)


def solution(mesh):
    in_specs = (
        P(None, "gx", "gy"),
        P(None, None, "gx", "gy"),
        P(None, "gx", "gy"),
        P(None, "gx", "gy"),
        P(),
        P(),
        P(None, "gx", "gy"),
    )
    out_specs = (P(None, "gx", "gy"), P(None, "gx", "gy"))
    return jax.shard_map(
        on_device, mesh=mesh, in_specs=in_specs, out_specs=out_specs, check_vma=False
    )
```
